256 devices in a mesh: gx: 8 (over x, core), gy: 8 (over z), gz: 4 (over y).
Axes of the slice: x: 4, y: 4, z: 8, core: 2. Of those that a mesh axis runs over, the one named last changes fastest.
Arguments:
- orbitals: float32 [32, 64, 128, 512], P(None, 'gx', 'gy', 'gz'), may hold values from -12 to 12
- potential: float32 [64, 128, 512], P('gx', 'gy', 'gz'), may hold values from -1 to 1
Outputs:
- filtered_basis: float32 [32, 64, 128, 512], P(None, 'gx', 'gy', 'gz')
- r_factor: float32 [32, 32], replicated
The draws below stay inside these ranges and needn't reach their ends.
All inputs are finite; a program needn't handle non-finite values.
Results may differ from the reference program's by a relative error of at most 0.00013.
Values sent between devices are 32-bit elements; how exact they have to be, the bound alone decides.
No kernel may reach another device: no remote copies, remote signals or barrier semaphores. Data moves between devices by JAX's collectives and lax.ppermute only.
A program may use at most 128 MiB of HBM per device.

```python
import jax
import jax.numpy as jnp
from jax import lax

NORB = 32
CX = 8
CY = 16
CZ = 128
NX = 64
NY = 128
NZ = 512


def draw_orbitals(key, part):
    bricks_x = NX // CX
    bricks_y = NY // CY
    bricks_z = NZ // CZ
    keys = jax.random.split(key, 6)
    table_shape = (NORB, bricks_x, 1, bricks_y, 1, bricks_z, 1)
    brick_scale = jnp.exp(jax.random.uniform(keys[0], table_shape, jnp.float32, -1.0, 1.0))
    group_mix = jax.random.uniform(keys[1], table_shape, jnp.float32, 0.3, 0.8)
    shared_mix = jax.random.uniform(keys[2], table_shape, jnp.float32, -0.6, 0.6)
    cell_shape = (bricks_x, CX, bricks_y, CY, bricks_z, CZ)
    own_part = jax.random.truncated_normal(keys[3], -3.0, 3.0, (NORB,) + cell_shape, jnp.float32)
    group_part = jax.random.truncated_normal(keys[4], -3.0, 3.0, (4,) + cell_shape, jnp.float32)
    shared_part = jax.random.truncated_normal(keys[5], -3.0, 3.0, (1,) + cell_shape, jnp.float32)
    group_full = jnp.tile(group_part, (NORB // 4, 1, 1, 1, 1, 1, 1))
    inner = own_part + group_mix * group_full + shared_mix * shared_part
    across = jnp.arange(NX, dtype=jnp.float32) / max(NX - 1, 1)
    envelope = (1.0 + 2.0 * across).reshape(1, bricks_x, CX, 1, 1, 1, 1)
    values = jnp.clip(0.5 * envelope * brick_scale * inner, -12.0, 12.0)
    return values.reshape(NORB, NX, NY, NZ).astype(jnp.float32)


def levels(rng, extent, cuts, low, high):
    factor_of = 1.0
    for position, parts in cuts:
        steps = jax.random.uniform(jax.random.fold_in(jax.random.fold_in(rng, 6), position), (parts,), jnp.float32, low / len(cuts), high / len(cuts))
        factor_of = factor_of * jnp.repeat(jnp.exp(steps), extent[position] // parts).reshape((-1,) + (1,) * (len(extent) - 1 - position))
    return factor_of


def setup_inputs(seed: int = 0) -> dict:
    streams_of = jax.random.split(jax.random.key(seed), 3)
    return {
        "orbitals": draw_orbitals(jax.random.fold_in(streams_of[2], 71), 0),
        "potential": jnp.clip(jax.random.uniform(streams_of[1], (NX, NY, NZ), jnp.float32, -1.0, 1.0) * levels(streams_of[1], (NX, NY, NZ), ((0, 8), (1, 8), (2, 4)), -0.4, 0.0), -1.0, 1.0),
    }


TAPS = (-1.0 / 12.0, 4.0 / 3.0, -2.5, 4.0 / 3.0, -1.0 / 12.0)

def laplacian(field):
    summed = 3.0 * TAPS[2] * field
    for axis_id in range(3):
        for offset, weight in ((-2, TAPS[0]), (-1, TAPS[1]), (1, TAPS[3]), (2, TAPS[4])):
            summed = summed + weight * jnp.roll(field, -offset, axis=axis_id)
    return summed

def hamiltonian(field, potential):
    return -0.5 * laplacian(field) + potential * field

def filter_one(single, potential):
    first = (hamiltonian(single, potential) - 5.5 * single) / 3.5
    return 2.0 * (hamiltonian(first, potential) - 5.5 * first) / 3.5 - single

def reference(orbitals, potential):
    second = lax.map(lambda single: filter_one(single, potential), orbitals)
    norb_count = orbitals.shape[0]
    filtered = second.reshape(norb_count, -1)
    cells = filtered.shape[1]
    correlation = jnp.dot(filtered, filtered.T, precision=lax.Precision.HIGHEST) / cells
    lower = jnp.linalg.cholesky(correlation)
    basis = jax.scipy.linalg.solve_triangular(lower, filtered, lower=True)
    return (basis.reshape(orbitals.shape), lower.T)
```

```python
import jax
import jax.numpy as jnp
from jax import lax
from jax.sharding import PartitionSpec as P

TAPS = (-1.0 / 12.0, 4.0 / 3.0, -2.5, 4.0 / 3.0, -1.0 / 12.0)
AXES = ("gx", "gy", "gz")


def shift_pairs(n, step):
    return [(i, (i + step) % n) for i in range(n)]


def halos(f):
    out = {}
    for axis, dim in (("gx", 1), ("gy", 2), ("gz", 3)):
        n, length = lax.axis_size(axis), f.shape[dim]
        last = lax.slice_in_dim(f, length - 2, length, axis=dim)
        first = lax.slice_in_dim(f, 0, 2, axis=dim)
        if dim == 3:
            shape = last.shape
            pack = lambda a: jnp.transpose(a, (0, 3, 1, 2)).reshape(shape[0] * 2, -1)
            unpack = lambda a: jnp.transpose(a.reshape(shape[0], 2, shape[1], shape[2]), (0, 2, 3, 1))
            before = unpack(lax.ppermute(pack(last), axis, shift_pairs(n, 1)))
            after = unpack(lax.ppermute(pack(first), axis, shift_pairs(n, -1)))
        else:
            before = lax.ppermute(last, axis, shift_pairs(n, 1))
            after = lax.ppermute(first, axis, shift_pairs(n, -1))
        out[dim] = (before, after)
    return out


def laplacian(f, rims):
    summed = 3.0 * TAPS[2] * f
    for dim in (1, 2, 3):
        before, after = rims[dim]
        ext = jnp.concatenate([before, f, after], axis=dim)
        length = f.shape[dim]
        for offset, weight in ((-2, TAPS[0]), (-1, TAPS[1]), (1, TAPS[3]), (2, TAPS[4])):
            summed = summed + weight * lax.slice_in_dim(ext, 2 + offset, 2 + offset + length, axis=dim)
    return summed


def hamiltonian(f, potential_cube):
    return -0.5 * laplacian(f, halos(f)) + potential_cube * f


def butterfly_sum(c):
    for axis in ("gz", "gy", "gx"):
        n = lax.axis_size(axis)
        d = 1
        while d < n:
            c = c + lax.ppermute(c, axis, [(i, i ^ d) for i in range(n)])
            d *= 2
    return c


def per_device(orbitals, potential):
    potential_cube = potential[None]
    first = (hamiltonian(orbitals, potential_cube) - 5.5 * orbitals) / 3.5
    second = 2.0 * (hamiltonian(first, potential_cube) - 5.5 * first) / 3.5 - orbitals
    norb_count = orbitals.shape[0]
    filtered = second.reshape(norb_count, -1)
    all_cells = filtered.shape[1] * lax.axis_size("gx") * lax.axis_size("gy") * lax.axis_size("gz")
    correlation = jnp.dot(filtered, filtered.T, precision=lax.Precision.HIGHEST) / all_cells
    lower = jnp.linalg.cholesky(butterfly_sum(correlation))
    eye = jnp.eye(norb_count, dtype=lower.dtype)
    inverse = jax.scipy.linalg.solve_triangular(lower, eye, lower=True)
    basis = jnp.dot(inverse, filtered, precision=lax.Precision.HIGHEST)
    return (basis.reshape(orbitals.shape), lower.T)


def solution(mesh):
    in_specs = (P(None, "gx", "gy", "gz"), P("gx", "gy", "gz"))
    out_specs = (P(None, "gx", "gy", "gz"), P())
    return jax.shard_map(
        per_device, mesh=mesh, in_specs=in_specs, out_specs=out_specs, check_vma=False
    )
```

```python
import functools

import jax
import jax.numpy as jnp
from jax import lax
from jax.experimental import pallas as pl
from jax.experimental.pallas import tpu as pltpu
from jax.sharding import PartitionSpec as P

TAPS = (-1.0 / 12.0, 4.0 / 3.0, -2.5, 4.0 / 3.0, -1.0 / 12.0)
BLOCK = 4
INTERPRET = False
HI = lax.Precision.HIGHEST


def shift_pairs(n, step):
    return [(i, (i + step) % n) for i in range(n)]


def face_selector(rows, lanes):
    r = lax.broadcasted_iota(jnp.int32, (rows, lanes), 0)
    l = lax.broadcasted_iota(jnp.int32, (rows, lanes), 1)
    pick = ((r < 2) & (l == r)) | ((r >= 2) & (r < 4) & (l == r + lanes - 4))
    return jnp.where(pick, 1.0, 0.0).astype(jnp.float32)


def placer(rows, lanes, low_side):
    r = lax.broadcasted_iota(jnp.int32, (rows, lanes), 0)
    l = lax.broadcasted_iota(jnp.int32, (rows, lanes), 1)
    if low_side:
        pick = ((r == 2) & (l == 0)) | ((r == 3) & (l == 1))
    else:
        pick = ((r == 0) & (l == lanes - 2)) | ((r == 1) & (l == lanes - 1))
    return jnp.where(pick, 1.0, 0.0).astype(jnp.float32)


def faces_of(plane, selector):
    return lax.dot_general(selector, plane, (((1,), (1,)), ((), ())), precision=HI,
                           preferred_element_type=jnp.float32)


def stage_kernel(*refs, last):
    if last:
        (f_ref, xlo_ref, xhi_ref, ylo_ref, yhi_ref, zlo_ref, zhi_ref, pot_ref, orb_ref,
         out_ref) = refs
    else:
        (f_ref, xlo_ref, xhi_ref, ylo_ref, yhi_ref, zlo_ref, zhi_ref, pot_ref,
         out_ref, face_ref) = refs
    nb, cx, cy, cz = f_ref.shape
    rows = cx * cy
    frows = zlo_ref.shape[1]
    t_lo = placer(frows, cz, True)
    t_hi = placer(frows, cz, False)
    sel = face_selector(frows, cz)
    lane = lax.broadcasted_iota(jnp.int32, (rows, cz), 1)
    yid = lax.broadcasted_iota(jnp.int32, (cx, cy, cz), 1)
    pot = pot_ref[...]
    tn = (((0,), (0,)), ((), ()))
    for b in range(nb):
        f3 = f_ref[b]
        summed = 3.0 * TAPS[2] * f3
        ext = jnp.concatenate([xlo_ref[b], f3, xhi_ref[b]], axis=0)
        for offset, weight in ((-2, TAPS[0]), (-1, TAPS[1]), (1, TAPS[3]), (2, TAPS[4])):
            summed = summed + weight * ext[2 + offset: 2 + offset + cx]
        ylo = ylo_ref[b]
        yhi = yhi_ref[b]
        ym2 = jnp.where(yid == 0, ylo[:, 0:1, :], jnp.where(yid == 1, ylo[:, 1:2, :], pltpu.roll(f3, 2, 1)))
        ym1 = jnp.where(yid == 0, ylo[:, 1:2, :], pltpu.roll(f3, 1, 1))
        yp1 = jnp.where(yid == cy - 1, yhi[:, 0:1, :], pltpu.roll(f3, cy - 1, 1))
        yp2 = jnp.where(yid == cy - 2, yhi[:, 0:1, :], jnp.where(yid == cy - 1, yhi[:, 1:2, :], pltpu.roll(f3, cy - 2, 1)))
        for shifted, weight in ((ym2, TAPS[0]), (ym1, TAPS[1]), (yp1, TAPS[3]), (yp2, TAPS[4])):
            summed = summed + weight * shifted
        f2 = f3.reshape(rows, cz)
        zl = lax.dot_general(zlo_ref[b], t_lo, tn, precision=HI, preferred_element_type=jnp.float32)
        zh = lax.dot_general(zhi_ref[b], t_hi, tn, precision=HI, preferred_element_type=jnp.float32)
        zm2 = jnp.where(lane < 2, zl, pltpu.roll(f2, 2, 1))
        zm1 = jnp.where(lane < 1, pltpu.roll(zl, cz - 1, 1), pltpu.roll(f2, 1, 1))
        zp1 = jnp.where(lane >= cz - 1, pltpu.roll(zh, 1, 1), pltpu.roll(f2, cz - 1, 1))
        zp2 = jnp.where(lane >= cz - 2, zh, pltpu.roll(f2, cz - 2, 1))
        summed = summed.reshape(rows, cz)
        for shifted, weight in ((zm2, TAPS[0]), (zm1, TAPS[1]), (zp1, TAPS[3]), (zp2, TAPS[4])):
            summed = summed + weight * shifted
        pot2 = pot.reshape(rows, cz)
        h = -0.5 * summed + pot2 * f2
        if last:
            res = 2.0 * (h - 5.5 * f2) / 3.5 - orb_ref[b].reshape(rows, cz)
        else:
            res = (h - 5.5 * f2) / 3.5
            face_ref[b] = faces_of(res, sel)
        out_ref[b] = res.reshape(cx, cy, cz)


def z_face_kernel(f_ref, face_ref):
    nb, cx, cy, cz = f_ref.shape
    sel = face_selector(face_ref.shape[1], cz)
    for b in range(nb):
        face_ref[b] = faces_of(f_ref[b].reshape(cx * cy, cz), sel)


def z_faces(f):
    norb, cx, cy, cz = f.shape
    blk = pl.BlockSpec((BLOCK, cx, cy, cz), lambda i: (i, 0, 0, 0))
    fblk = pl.BlockSpec((BLOCK, 8, cx * cy), lambda i: (i, 0, 0))
    return pl.pallas_call(
        z_face_kernel, grid=(norb // BLOCK,), in_specs=[blk], out_specs=fblk,
        out_shape=jax.ShapeDtypeStruct((norb, 8, cx * cy), jnp.float32), interpret=INTERPRET,
    )(f)


def exchange(f, zface):
    out = []
    for axis, dim in (("gx", 1), ("gy", 2)):
        n, length = lax.axis_size(axis), f.shape[dim]
        last = lax.slice_in_dim(f, length - 2, length, axis=dim)
        first = lax.slice_in_dim(f, 0, 2, axis=dim)
        out.append(lax.ppermute(last, axis, shift_pairs(n, 1)))
        out.append(lax.ppermute(first, axis, shift_pairs(n, -1)))
    n = lax.axis_size("gz")
    out.append(lax.ppermute(zface, "gz", shift_pairs(n, 1)))
    out.append(lax.ppermute(zface, "gz", shift_pairs(n, -1)))
    return out


def stage(f, rims, potential, orbitals=None):
    norb, cx, cy, cz = f.shape
    last = orbitals is not None
    blk = pl.BlockSpec((BLOCK, cx, cy, cz), lambda i: (i, 0, 0, 0))
    xblk = pl.BlockSpec((BLOCK, 2, cy, cz), lambda i: (i, 0, 0, 0))
    yblk = pl.BlockSpec((BLOCK, cx, 2, cz), lambda i: (i, 0, 0, 0))
    fblk = pl.BlockSpec((BLOCK, 8, cx * cy), lambda i: (i, 0, 0))
    pblk = pl.BlockSpec((cx, cy, cz), lambda i: (0, 0, 0))
    in_specs = [blk, xblk, xblk, yblk, yblk, fblk, fblk, pblk]
    args = [f, *rims, potential]
    if last:
        in_specs.append(blk)
        args.append(orbitals)
        out_specs = blk
        out_shape = jax.ShapeDtypeStruct(f.shape, jnp.float32)
    else:
        out_specs = (blk, fblk)
        out_shape = (jax.ShapeDtypeStruct(f.shape, jnp.float32),
                     jax.ShapeDtypeStruct((norb, 8, cx * cy), jnp.float32))
    return pl.pallas_call(
        functools.partial(stage_kernel, last=last), grid=(norb // BLOCK,), in_specs=in_specs,
        out_specs=out_specs, out_shape=out_shape, interpret=INTERPRET,
        compiler_params=pltpu.CompilerParams(dimension_semantics=("arbitrary",)),
    )(*args)


def butterfly_sum(c):
    for axis in ("gz", "gy", "gx"):
        n = lax.axis_size(axis)
        d = 1
        while d < n:
            c = c + lax.ppermute(c, axis, [(i, i ^ d) for i in range(n)])
            d *= 2
    return c


def per_device(orbitals, potential):
    first, first_z = stage(orbitals, exchange(orbitals, z_faces(orbitals)), potential)
    second = stage(first, exchange(first, first_z), potential, orbitals)
    norb_count = orbitals.shape[0]
    filtered = second.reshape(norb_count, -1)
    all_cells = filtered.shape[1] * lax.axis_size("gx") * lax.axis_size("gy") * lax.axis_size("gz")
    correlation = jnp.dot(filtered, filtered.T, precision=HI) / all_cells
    lower = jnp.linalg.cholesky(butterfly_sum(correlation))
    eye = jnp.eye(norb_count, dtype=lower.dtype)
    inverse = jax.scipy.linalg.solve_triangular(lower, eye, lower=True)
    basis = jnp.dot(inverse, filtered, precision=HI)
    return (basis.reshape(orbitals.shape), lower.T)


def solution(mesh):
    in_specs = (P(None, "gx", "gy", "gz"), P("gx", "gy", "gz"))
    out_specs = (P(None, "gx", "gy", "gz"), P())
    return jax.shard_map(
        per_device, mesh=mesh, in_specs=in_specs, out_specs=out_specs, check_vma=False
    )
```

```python
import functools

import jax
import jax.numpy as jnp
from jax import lax
from jax.experimental import pallas as pl
from jax.experimental.pallas import tpu as pltpu
from jax.sharding import PartitionSpec as P

TAPS = (-1.0 / 12.0, 4.0 / 3.0, -2.5, 4.0 / 3.0, -1.0 / 12.0)
BLOCK = 4
INTERPRET = False
HI = lax.Precision.HIGHEST


def shift_pairs(n, step):
    return [(i, (i + step) % n) for i in range(n)]


def faces_of(plane):
    return jnp.transpose(pltpu.roll(plane, 2, 1))[0:8]


def halo_image(zlo, zhi):
    rows = zlo.shape[1]
    pad = jnp.zeros((rows - 2 * zlo.shape[0], rows), jnp.float32)
    return jnp.transpose(jnp.concatenate([zlo, zhi, pad], axis=0))


def stage_kernel(*refs, last):
    if last:
        (f_ref, xlo_ref, xhi_ref, ylo_ref, yhi_ref, zlo_ref, zhi_ref, pot_ref, orb_ref,
         out_ref) = refs
    else:
        (f_ref, xlo_ref, xhi_ref, ylo_ref, yhi_ref, zlo_ref, zhi_ref, pot_ref,
         out_ref, face_ref) = refs
    nb, cx, cy, cz = f_ref.shape
    rows = cx * cy
    lane = lax.broadcasted_iota(jnp.int32, (rows, cz), 1)
    yid = lax.broadcasted_iota(jnp.int32, (cx, cy, cz), 1)
    pot = pot_ref[...]
    for b in range(nb):
        f3 = f_ref[b]
        summed = 3.0 * TAPS[2] * f3
        ext = jnp.concatenate([xlo_ref[b], f3, xhi_ref[b]], axis=0)
        for offset, weight in ((-2, TAPS[0]), (-1, TAPS[1]), (1, TAPS[3]), (2, TAPS[4])):
            summed = summed + weight * ext[2 + offset: 2 + offset + cx]
        ylo = ylo_ref[b]
        yhi = yhi_ref[b]
        ym2 = jnp.where(yid == 0, ylo[:, 0:1, :], jnp.where(yid == 1, ylo[:, 1:2, :], pltpu.roll(f3, 2, 1)))
        ym1 = jnp.where(yid == 0, ylo[:, 1:2, :], pltpu.roll(f3, 1, 1))
        yp1 = jnp.where(yid == cy - 1, yhi[:, 0:1, :], pltpu.roll(f3, cy - 1, 1))
        yp2 = jnp.where(yid == cy - 2, yhi[:, 0:1, :], jnp.where(yid == cy - 1, yhi[:, 1:2, :], pltpu.roll(f3, cy - 2, 1)))
        for shifted, weight in ((ym2, TAPS[0]), (ym1, TAPS[1]), (yp1, TAPS[3]), (yp2, TAPS[4])):
            summed = summed + weight * shifted
        f2 = f3.reshape(rows, cz)
        zim = halo_image(zlo_ref[b], zhi_ref[b])
        zm2 = jnp.where(lane < 2, zim, pltpu.roll(f2, 2, 1))
        zm1 = jnp.where(lane < 1, pltpu.roll(zim, cz - 1, 1), pltpu.roll(f2, 1, 1))
        zp1 = jnp.where(lane >= cz - 1, pltpu.roll(zim, cz - 11, 1), pltpu.roll(f2, cz - 1, 1))
        zp2 = jnp.where(lane >= cz - 2, pltpu.roll(zim, cz - 12, 1), pltpu.roll(f2, cz - 2, 1))
        summed = summed.reshape(rows, cz)
        for shifted, weight in ((zm2, TAPS[0]), (zm1, TAPS[1]), (zp1, TAPS[3]), (zp2, TAPS[4])):
            summed = summed + weight * shifted
        pot2 = pot.reshape(rows, cz)
        h = -0.5 * summed + pot2 * f2
        if last:
            res = 2.0 * (h - 5.5 * f2) / 3.5 - orb_ref[b].reshape(rows, cz)
        else:
            res = (h - 5.5 * f2) / 3.5
            face_ref[b] = faces_of(res)
        out_ref[b] = res.reshape(cx, cy, cz)


def z_face_kernel(f_ref, face_ref):
    nb, cx, cy, cz = f_ref.shape
    for b in range(nb):
        face_ref[b] = faces_of(f_ref[b].reshape(cx * cy, cz))


def z_faces(f):
    norb, cx, cy, cz = f.shape
    blk = pl.BlockSpec((BLOCK, cx, cy, cz), lambda i: (i, 0, 0, 0))
    fblk = pl.BlockSpec((BLOCK, 8, cx * cy), lambda i: (i, 0, 0))
    return pl.pallas_call(
        z_face_kernel, grid=(norb // BLOCK,), in_specs=[blk], out_specs=fblk,
        out_shape=jax.ShapeDtypeStruct((norb, 8, cx * cy), jnp.float32), interpret=INTERPRET,
    )(f)


def exchange(f, zface):
    out = []
    for axis, dim in (("gx", 1), ("gy", 2)):
        n, length = lax.axis_size(axis), f.shape[dim]
        last = lax.slice_in_dim(f, length - 2, length, axis=dim)
        first = lax.slice_in_dim(f, 0, 2, axis=dim)
        out.append(lax.ppermute(last, axis, shift_pairs(n, 1)))
        out.append(lax.ppermute(first, axis, shift_pairs(n, -1)))
    n = lax.axis_size("gz")
    out.append(lax.ppermute(zface, "gz", shift_pairs(n, 1)))
    out.append(lax.ppermute(zface, "gz", shift_pairs(n, -1)))
    return out


def stage(f, rims, potential, orbitals=None):
    norb, cx, cy, cz = f.shape
    last = orbitals is not None
    blk = pl.BlockSpec((BLOCK, cx, cy, cz), lambda i: (i, 0, 0, 0))
    xblk = pl.BlockSpec((BLOCK, 2, cy, cz), lambda i: (i, 0, 0, 0))
    yblk = pl.BlockSpec((BLOCK, cx, 2, cz), lambda i: (i, 0, 0, 0))
    fblk = pl.BlockSpec((BLOCK, 8, cx * cy), lambda i: (i, 0, 0))
    pblk = pl.BlockSpec((cx, cy, cz), lambda i: (0, 0, 0))
    in_specs = [blk, xblk, xblk, yblk, yblk, fblk, fblk, pblk]
    args = [f, *rims, potential]
    if last:
        in_specs.append(blk)
        args.append(orbitals)
        out_specs = blk
        out_shape = jax.ShapeDtypeStruct(f.shape, jnp.float32)
    else:
        out_specs = (blk, fblk)
        out_shape = (jax.ShapeDtypeStruct(f.shape, jnp.float32),
                     jax.ShapeDtypeStruct((norb, 8, cx * cy), jnp.float32))
    return pl.pallas_call(
        functools.partial(stage_kernel, last=last), grid=(norb // BLOCK,), in_specs=in_specs,
        out_specs=out_specs, out_shape=out_shape, interpret=INTERPRET,
        compiler_params=pltpu.CompilerParams(dimension_semantics=("arbitrary",)),
    )(*args)


def butterfly_sum(c):
    for axis in ("gz", "gy", "gx"):
        n = lax.axis_size(axis)
        d = 1
        while d < n:
            c = c + lax.ppermute(c, axis, [(i, i ^ d) for i in range(n)])
            d *= 2
    return c


def per_device(orbitals, potential):
    first, first_z = stage(orbitals, exchange(orbitals, z_faces(orbitals)), potential)
    second = stage(first, exchange(first, first_z), potential, orbitals)
    norb_count = orbitals.shape[0]
    filtered = second.reshape(norb_count, -1)
    all_cells = filtered.shape[1] * lax.axis_size("gx") * lax.axis_size("gy") * lax.axis_size("gz")
    correlation = jnp.dot(filtered, filtered.T, precision=HI) / all_cells
    lower = jnp.linalg.cholesky(butterfly_sum(correlation))
    eye = jnp.eye(norb_count, dtype=lower.dtype)
    inverse = jax.scipy.linalg.solve_triangular(lower, eye, lower=True)
    basis = jnp.dot(inverse, filtered, precision=HI)
    return (basis.reshape(orbitals.shape), lower.T)


def solution(mesh):
    in_specs = (P(None, "gx", "gy", "gz"), P("gx", "gy", "gz"))
    out_specs = (P(None, "gx", "gy", "gz"), P())
    return jax.shard_map(
        per_device, mesh=mesh, in_specs=in_specs, out_specs=out_specs, check_vma=False
    )
```

```python
import functools

import jax
import jax.numpy as jnp
from jax import lax
from jax.experimental import pallas as pl
from jax.experimental.pallas import tpu as pltpu
from jax.sharding import PartitionSpec as P

TAPS = (-1.0 / 12.0, 4.0 / 3.0, -2.5, 4.0 / 3.0, -1.0 / 12.0)
BLOCK = 8
INTERPRET = False
HI = lax.Precision.HIGHEST


def shift_pairs(n, step):
    return [(i, (i + step) % n) for i in range(n)]


def faces_of(plane):
    return jnp.transpose(pltpu.roll(plane, 2, 1))[0:8]


def halo_image(zlo, zhi):
    rows = zlo.shape[1]
    pad = jnp.zeros((rows - 2 * zlo.shape[0], rows), jnp.float32)
    return jnp.transpose(jnp.concatenate([zlo, zhi, pad], axis=0))


def stage_kernel(*refs, last):
    if last:
        (f_ref, xlo_ref, xhi_ref, ylo_ref, yhi_ref, zlo_ref, zhi_ref, pot_ref, orb_ref,
         out_ref) = refs
    else:
        (f_ref, xlo_ref, xhi_ref, ylo_ref, yhi_ref, zlo_ref, zhi_ref, pot_ref,
         out_ref, face_ref) = refs
    nb, cx, cy, cz = f_ref.shape
    rows = cx * cy
    lane = lax.broadcasted_iota(jnp.int32, (rows, cz), 1)
    yid = lax.broadcasted_iota(jnp.int32, (cx, cy, cz), 1)
    pot = pot_ref[...]
    for b in range(nb):
        f3 = f_ref[b]
        summed = 3.0 * TAPS[2] * f3
        ext = jnp.concatenate([xlo_ref[b], f3, xhi_ref[b]], axis=0)
        for offset, weight in ((-2, TAPS[0]), (-1, TAPS[1]), (1, TAPS[3]), (2, TAPS[4])):
            summed = summed + weight * ext[2 + offset: 2 + offset + cx]
        ylo = ylo_ref[b]
        yhi = yhi_ref[b]
        ym2 = jnp.where(yid == 0, ylo[:, 0:1, :], jnp.where(yid == 1, ylo[:, 1:2, :], pltpu.roll(f3, 2, 1)))
        ym1 = jnp.where(yid == 0, ylo[:, 1:2, :], pltpu.roll(f3, 1, 1))
        yp1 = jnp.where(yid == cy - 1, yhi[:, 0:1, :], pltpu.roll(f3, cy - 1, 1))
        yp2 = jnp.where(yid == cy - 2, yhi[:, 0:1, :], jnp.where(yid == cy - 1, yhi[:, 1:2, :], pltpu.roll(f3, cy - 2, 1)))
        for shifted, weight in ((ym2, TAPS[0]), (ym1, TAPS[1]), (yp1, TAPS[3]), (yp2, TAPS[4])):
            summed = summed + weight * shifted
        f2 = f3.reshape(rows, cz)
        zim = halo_image(zlo_ref[b], zhi_ref[b])
        zm2 = jnp.where(lane < 2, zim, pltpu.roll(f2, 2, 1))
        zm1 = jnp.where(lane < 1, pltpu.roll(zim, cz - 1, 1), pltpu.roll(f2, 1, 1))
        zp1 = jnp.where(lane >= cz - 1, pltpu.roll(zim, cz - 11, 1), pltpu.roll(f2, cz - 1, 1))
        zp2 = jnp.where(lane >= cz - 2, pltpu.roll(zim, cz - 12, 1), pltpu.roll(f2, cz - 2, 1))
        summed = summed.reshape(rows, cz)
        for shifted, weight in ((zm2, TAPS[0]), (zm1, TAPS[1]), (zp1, TAPS[3]), (zp2, TAPS[4])):
            summed = summed + weight * shifted
        pot2 = pot.reshape(rows, cz)
        h = -0.5 * summed + pot2 * f2
        if last:
            res = 2.0 * (h - 5.5 * f2) / 3.5 - orb_ref[b].reshape(rows, cz)
        else:
            res = (h - 5.5 * f2) / 3.5
            face_ref[b] = faces_of(res)
        out_ref[b] = res.reshape(cx, cy, cz)


def z_face_kernel(f_ref, face_ref):
    nb, cx, cy, cz = f_ref.shape
    for b in range(nb):
        face_ref[b] = faces_of(f_ref[b].reshape(cx * cy, cz))


def z_faces(f):
    norb, cx, cy, cz = f.shape
    blk = pl.BlockSpec((BLOCK, cx, cy, cz), lambda i: (i, 0, 0, 0))
    fblk = pl.BlockSpec((BLOCK, 8, cx * cy), lambda i: (i, 0, 0))
    return pl.pallas_call(
        z_face_kernel, grid=(norb // BLOCK,), in_specs=[blk], out_specs=fblk,
        out_shape=jax.ShapeDtypeStruct((norb, 8, cx * cy), jnp.float32), interpret=INTERPRET,
    )(f)


def exchange(f, zface):
    out = []
    for axis, dim in (("gx", 1), ("gy", 2)):
        n, length = lax.axis_size(axis), f.shape[dim]
        last = lax.slice_in_dim(f, length - 2, length, axis=dim)
        first = lax.slice_in_dim(f, 0, 2, axis=dim)
        out.append(lax.ppermute(last, axis, shift_pairs(n, 1)))
        out.append(lax.ppermute(first, axis, shift_pairs(n, -1)))
    n = lax.axis_size("gz")
    out.append(lax.ppermute(zface, "gz", shift_pairs(n, 1)))
    out.append(lax.ppermute(zface, "gz", shift_pairs(n, -1)))
    return out


def stage(f, rims, potential, orbitals=None):
    norb, cx, cy, cz = f.shape
    last = orbitals is not None
    blk = pl.BlockSpec((BLOCK, cx, cy, cz), lambda i: (i, 0, 0, 0))
    xblk = pl.BlockSpec((BLOCK, 2, cy, cz), lambda i: (i, 0, 0, 0))
    yblk = pl.BlockSpec((BLOCK, cx, 2, cz), lambda i: (i, 0, 0, 0))
    fblk = pl.BlockSpec((BLOCK, 8, cx * cy), lambda i: (i, 0, 0))
    pblk = pl.BlockSpec((cx, cy, cz), lambda i: (0, 0, 0))
    in_specs = [blk, xblk, xblk, yblk, yblk, fblk, fblk, pblk]
    args = [f, *rims, potential]
    if last:
        in_specs.append(blk)
        args.append(orbitals)
        out_specs = blk
        out_shape = jax.ShapeDtypeStruct(f.shape, jnp.float32)
    else:
        out_specs = (blk, fblk)
        out_shape = (jax.ShapeDtypeStruct(f.shape, jnp.float32),
                     jax.ShapeDtypeStruct((norb, 8, cx * cy), jnp.float32))
    return pl.pallas_call(
        functools.partial(stage_kernel, last=last), grid=(norb // BLOCK,), in_specs=in_specs,
        out_specs=out_specs, out_shape=out_shape, interpret=INTERPRET,
        compiler_params=pltpu.CompilerParams(dimension_semantics=("arbitrary",)),
    )(*args)


def butterfly_sum(c):
    for axis in ("gz", "gy", "gx"):
        n = lax.axis_size(axis)
        d = 1
        while d < n:
            c = c + lax.ppermute(c, axis, [(i, i ^ d) for i in range(n)])
            d *= 2
    return c


def per_device(orbitals, potential):
    first, first_z = stage(orbitals, exchange(orbitals, z_faces(orbitals)), potential)
    second = stage(first, exchange(first, first_z), potential, orbitals)
    norb_count = orbitals.shape[0]
    all_cells = second[0].size * lax.axis_size("gx") * lax.axis_size("gy") * lax.axis_size("gz")
    correlation = jnp.einsum("axyz,bxyz->ab", second, second, precision=HI) / all_cells
    lower = jnp.linalg.cholesky(butterfly_sum(correlation))
    eye = jnp.eye(norb_count, dtype=lower.dtype)
    inverse = jax.scipy.linalg.solve_triangular(lower, eye, lower=True)
    basis = jnp.einsum("ab,bxyz->axyz", inverse, second, precision=HI)
    return (basis, lower.T)


def solution(mesh):
    in_specs = (P(None, "gx", "gy", "gz"), P("gx", "gy", "gz"))
    out_specs = (P(None, "gx", "gy", "gz"), P())
    return jax.shard_map(
        per_device, mesh=mesh, in_specs=in_specs, out_specs=out_specs, check_vma=False
    )
```

```python
import functools

import jax
import jax.numpy as jnp
from jax import lax
from jax.experimental import pallas as pl
from jax.experimental.pallas import tpu as pltpu
from jax.sharding import PartitionSpec as P

TAPS = (-1.0 / 12.0, 4.0 / 3.0, -2.5, 4.0 / 3.0, -1.0 / 12.0)
BLOCK = 8
CHUNKS = 2
INTERPRET = False
HI = lax.Precision.HIGHEST


def shift_pairs(n, step):
    return [(i, (i + step) % n) for i in range(n)]


def faces_of(plane):
    return jnp.transpose(pltpu.roll(plane, 2, 1))[0:8]


def halo_image(zlo, zhi):
    rows = zlo.shape[1]
    pad = jnp.zeros((rows - 2 * zlo.shape[0], rows), jnp.float32)
    return jnp.transpose(jnp.concatenate([zlo, zhi, pad], axis=0))


def stage_kernel(*refs, last):
    if last:
        (f_ref, xlo_ref, xhi_ref, ylo_ref, yhi_ref, zlo_ref, zhi_ref, pot_ref, orb_ref,
         out_ref) = refs
    else:
        (f_ref, xlo_ref, xhi_ref, ylo_ref, yhi_ref, zlo_ref, zhi_ref, pot_ref,
         out_ref, face_ref) = refs
    nb, cx, cy, cz = f_ref.shape
    rows = cx * cy
    lane = lax.broadcasted_iota(jnp.int32, (rows, cz), 1)
    yid = lax.broadcasted_iota(jnp.int32, (cx, cy, cz), 1)
    pot = pot_ref[...]
    for b in range(nb):
        f3 = f_ref[b]
        summed = 3.0 * TAPS[2] * f3
        ext = jnp.concatenate([xlo_ref[b], f3, xhi_ref[b]], axis=0)
        for offset, weight in ((-2, TAPS[0]), (-1, TAPS[1]), (1, TAPS[3]), (2, TAPS[4])):
            summed = summed + weight * ext[2 + offset: 2 + offset + cx]
        ylo = ylo_ref[b]
        yhi = yhi_ref[b]
        ym2 = jnp.where(yid == 0, ylo[:, 0:1, :], jnp.where(yid == 1, ylo[:, 1:2, :], pltpu.roll(f3, 2, 1)))
        ym1 = jnp.where(yid == 0, ylo[:, 1:2, :], pltpu.roll(f3, 1, 1))
        yp1 = jnp.where(yid == cy - 1, yhi[:, 0:1, :], pltpu.roll(f3, cy - 1, 1))
        yp2 = jnp.where(yid == cy - 2, yhi[:, 0:1, :], jnp.where(yid == cy - 1, yhi[:, 1:2, :], pltpu.roll(f3, cy - 2, 1)))
        for shifted, weight in ((ym2, TAPS[0]), (ym1, TAPS[1]), (yp1, TAPS[3]), (yp2, TAPS[4])):
            summed = summed + weight * shifted
        f2 = f3.reshape(rows, cz)
        zim = halo_image(zlo_ref[b], zhi_ref[b])
        zm2 = jnp.where(lane < 2, zim, pltpu.roll(f2, 2, 1))
        zm1 = jnp.where(lane < 1, pltpu.roll(zim, cz - 1, 1), pltpu.roll(f2, 1, 1))
        zp1 = jnp.where(lane >= cz - 1, pltpu.roll(zim, cz - 11, 1), pltpu.roll(f2, cz - 1, 1))
        zp2 = jnp.where(lane >= cz - 2, pltpu.roll(zim, cz - 12, 1), pltpu.roll(f2, cz - 2, 1))
        summed = summed.reshape(rows, cz)
        for shifted, weight in ((zm2, TAPS[0]), (zm1, TAPS[1]), (zp1, TAPS[3]), (zp2, TAPS[4])):
            summed = summed + weight * shifted
        pot2 = pot.reshape(rows, cz)
        h = -0.5 * summed + pot2 * f2
        if last:
            res = 2.0 * (h - 5.5 * f2) / 3.5 - orb_ref[b].reshape(rows, cz)
        else:
            res = (h - 5.5 * f2) / 3.5
            face_ref[b] = faces_of(res)
        out_ref[b] = res.reshape(cx, cy, cz)


def z_face_kernel(f_ref, face_ref):
    nb, cx, cy, cz = f_ref.shape
    for b in range(nb):
        face_ref[b] = faces_of(f_ref[b].reshape(cx * cy, cz))


def z_faces(f):
    norb, cx, cy, cz = f.shape
    blk = pl.BlockSpec((BLOCK, cx, cy, cz), lambda i: (i, 0, 0, 0))
    fblk = pl.BlockSpec((BLOCK, 8, cx * cy), lambda i: (i, 0, 0))
    return pl.pallas_call(
        z_face_kernel, grid=(norb // BLOCK,), in_specs=[blk], out_specs=fblk,
        out_shape=jax.ShapeDtypeStruct((norb, 8, cx * cy), jnp.float32), interpret=INTERPRET,
    )(f)


def exchange(f, zface):
    out = []
    for axis, dim in (("gx", 1), ("gy", 2)):
        n, length = lax.axis_size(axis), f.shape[dim]
        last = lax.slice_in_dim(f, length - 2, length, axis=dim)
        first = lax.slice_in_dim(f, 0, 2, axis=dim)
        out.append(lax.ppermute(last, axis, shift_pairs(n, 1)))
        out.append(lax.ppermute(first, axis, shift_pairs(n, -1)))
    n = lax.axis_size("gz")
    out.append(lax.ppermute(zface, "gz", shift_pairs(n, 1)))
    out.append(lax.ppermute(zface, "gz", shift_pairs(n, -1)))
    return out


def stage(f, rims, potential, orbitals=None):
    norb, cx, cy, cz = f.shape
    last = orbitals is not None
    blk = pl.BlockSpec((BLOCK, cx, cy, cz), lambda i: (i, 0, 0, 0))
    xblk = pl.BlockSpec((BLOCK, 2, cy, cz), lambda i: (i, 0, 0, 0))
    yblk = pl.BlockSpec((BLOCK, cx, 2, cz), lambda i: (i, 0, 0, 0))
    fblk = pl.BlockSpec((BLOCK, 8, cx * cy), lambda i: (i, 0, 0))
    pblk = pl.BlockSpec((cx, cy, cz), lambda i: (0, 0, 0))
    in_specs = [blk, xblk, xblk, yblk, yblk, fblk, fblk, pblk]
    args = [f, *rims, potential]
    if last:
        in_specs.append(blk)
        args.append(orbitals)
        out_specs = blk
        out_shape = jax.ShapeDtypeStruct(f.shape, jnp.float32)
    else:
        out_specs = (blk, fblk)
        out_shape = (jax.ShapeDtypeStruct(f.shape, jnp.float32),
                     jax.ShapeDtypeStruct((norb, 8, cx * cy), jnp.float32))
    return pl.pallas_call(
        functools.partial(stage_kernel, last=last), grid=(norb // BLOCK,), in_specs=in_specs,
        out_specs=out_specs, out_shape=out_shape, interpret=INTERPRET,
        compiler_params=pltpu.CompilerParams(dimension_semantics=("arbitrary",)),
    )(*args)


def butterfly_sum(c):
    for axis in ("gz", "gy", "gx"):
        n = lax.axis_size(axis)
        d = 1
        while d < n:
            c = c + lax.ppermute(c, axis, [(i, i ^ d) for i in range(n)])
            d *= 2
    return c


def per_device(orbitals, potential):
    norb = orbitals.shape[0]
    step = norb // CHUNKS
    parts = [orbitals[c * step:(c + 1) * step] for c in range(CHUNKS)]
    rims = [exchange(part, z_faces(part)) for part in parts]
    firsts = [stage(part, rim, potential) for part, rim in zip(parts, rims)]
    rims = [exchange(first, first_z) for first, first_z in firsts]
    second = jnp.concatenate(
        [stage(first, rim, potential, part) for (first, _), rim, part in zip(firsts, rims, parts)], axis=0)
    norb_count = orbitals.shape[0]
    all_cells = second[0].size * lax.axis_size("gx") * lax.axis_size("gy") * lax.axis_size("gz")
    correlation = jnp.einsum("axyz,bxyz->ab", second, second, precision=HI) / all_cells
    lower = jnp.linalg.cholesky(butterfly_sum(correlation))
    eye = jnp.eye(norb_count, dtype=lower.dtype)
    inverse = jax.scipy.linalg.solve_triangular(lower, eye, lower=True)
    basis = jnp.einsum("ab,bxyz->axyz", inverse, second, precision=HI)
    return (basis, lower.T)


def solution(mesh):
    in_specs = (P(None, "gx", "gy", "gz"), P("gx", "gy", "gz"))
    out_specs = (P(None, "gx", "gy", "gz"), P())
    return jax.shard_map(
        per_device, mesh=mesh, in_specs=in_specs, out_specs=out_specs, check_vma=False
    )
```

```python
import functools

import jax
import jax.numpy as jnp
from jax import lax
from jax.experimental import pallas as pl
from jax.experimental.pallas import tpu as pltpu
from jax.sharding import PartitionSpec as P

TAPS = (-1.0 / 12.0, 4.0 / 3.0, -2.5, 4.0 / 3.0, -1.0 / 12.0)
BLOCK = 8
INTERPRET = False
HI = lax.Precision.HIGHEST


def shift_pairs(n, step):
    return [(i, (i + step) % n) for i in range(n)]


def faces_of(plane):
    return jnp.transpose(pltpu.roll(plane, 2, 1))[0:8]


def halo_image(zlo, zhi):
    rows = zlo.shape[1]
    pad = jnp.zeros((rows - 2 * zlo.shape[0], rows), jnp.float32)
    return jnp.transpose(jnp.concatenate([zlo, zhi, pad], axis=0))


def stage_kernel(*refs, last):
    if last:
        (f_ref, xlo_ref, xhi_ref, ylo_ref, yhi_ref, zlo_ref, zhi_ref, pot_ref, orb_ref,
         out_ref) = refs
    else:
        (f_ref, xlo_ref, xhi_ref, ylo_ref, yhi_ref, zlo_ref, zhi_ref, pot_ref,
         out_ref, face_ref) = refs
    nb, cx, cy, cz = f_ref.shape
    rows = cx * cy
    lane = lax.broadcasted_iota(jnp.int32, (rows, cz), 1)
    yid = lax.broadcasted_iota(jnp.int32, (cx, cy, cz), 1)
    pot = pot_ref[...]
    for b in range(nb):
        f3 = f_ref[b]
        summed = 3.0 * TAPS[2] * f3
        ext = jnp.concatenate([xlo_ref[b], f3, xhi_ref[b]], axis=0)
        for offset, weight in ((-2, TAPS[0]), (-1, TAPS[1]), (1, TAPS[3]), (2, TAPS[4])):
            summed = summed + weight * ext[2 + offset: 2 + offset + cx]
        ylo = ylo_ref[b]
        yhi = yhi_ref[b]
        ym2 = jnp.where(yid == 0, ylo[:, 0:1, :], jnp.where(yid == 1, ylo[:, 1:2, :], pltpu.roll(f3, 2, 1)))
        ym1 = jnp.where(yid == 0, ylo[:, 1:2, :], pltpu.roll(f3, 1, 1))
        yp1 = jnp.where(yid == cy - 1, yhi[:, 0:1, :], pltpu.roll(f3, cy - 1, 1))
        yp2 = jnp.where(yid == cy - 2, yhi[:, 0:1, :], jnp.where(yid == cy - 1, yhi[:, 1:2, :], pltpu.roll(f3, cy - 2, 1)))
        for shifted, weight in ((ym2, TAPS[0]), (ym1, TAPS[1]), (yp1, TAPS[3]), (yp2, TAPS[4])):
            summed = summed + weight * shifted
        f2 = f3.reshape(rows, cz)
        zim = halo_image(zlo_ref[b], zhi_ref[b])
        zm2 = jnp.where(lane < 2, zim, pltpu.roll(f2, 2, 1))
        zm1 = jnp.where(lane < 1, pltpu.roll(zim, cz - 1, 1), pltpu.roll(f2, 1, 1))
        zp1 = jnp.where(lane >= cz - 1, pltpu.roll(zim, cz - 11, 1), pltpu.roll(f2, cz - 1, 1))
        zp2 = jnp.where(lane >= cz - 2, pltpu.roll(zim, cz - 12, 1), pltpu.roll(f2, cz - 2, 1))
        summed = summed.reshape(rows, cz)
        for shifted, weight in ((zm2, TAPS[0]), (zm1, TAPS[1]), (zp1, TAPS[3]), (zp2, TAPS[4])):
            summed = summed + weight * shifted
        pot2 = pot.reshape(rows, cz)
        h = -0.5 * summed + pot2 * f2
        if last:
            res = 2.0 * (h - 5.5 * f2) / 3.5 - orb_ref[b].reshape(rows, cz)
        else:
            res = (h - 5.5 * f2) / 3.5
            face_ref[b] = faces_of(res)
        out_ref[b] = res.reshape(cx, cy, cz)


def z_face_kernel(f_ref, face_ref):
    nb, cx, cy, cz = f_ref.shape
    for b in range(nb):
        face_ref[b] = faces_of(f_ref[b].reshape(cx * cy, cz))


def z_faces(f):
    norb, cx, cy, cz = f.shape
    blk = pl.BlockSpec((BLOCK, cx, cy, cz), lambda i: (i, 0, 0, 0))
    fblk = pl.BlockSpec((BLOCK, 8, cx * cy), lambda i: (i, 0, 0))
    return pl.pallas_call(
        z_face_kernel, grid=(norb // BLOCK,), in_specs=[blk], out_specs=fblk,
        out_shape=jax.ShapeDtypeStruct((norb, 8, cx * cy), jnp.float32), interpret=INTERPRET,
    )(f)


def exchange(f, zface):
    out = []
    for axis, dim in (("gx", 1), ("gy", 2)):
        n, length = lax.axis_size(axis), f.shape[dim]
        last = lax.slice_in_dim(f, length - 2, length, axis=dim)
        first = lax.slice_in_dim(f, 0, 2, axis=dim)
        out.append(lax.ppermute(last, axis, shift_pairs(n, 1)))
        out.append(lax.ppermute(first, axis, shift_pairs(n, -1)))
    n = lax.axis_size("gz")
    out.append(lax.ppermute(zface, "gz", shift_pairs(n, 1)))
    out.append(lax.ppermute(zface, "gz", shift_pairs(n, -1)))
    return out


def stage(f, rims, potential, orbitals=None):
    norb, cx, cy, cz = f.shape
    last = orbitals is not None
    blk = pl.BlockSpec((BLOCK, cx, cy, cz), lambda i: (i, 0, 0, 0))
    xblk = pl.BlockSpec((BLOCK, 2, cy, cz), lambda i: (i, 0, 0, 0))
    yblk = pl.BlockSpec((BLOCK, cx, 2, cz), lambda i: (i, 0, 0, 0))
    fblk = pl.BlockSpec((BLOCK, 8, cx * cy), lambda i: (i, 0, 0))
    pblk = pl.BlockSpec((cx, cy, cz), lambda i: (0, 0, 0))
    in_specs = [blk, xblk, xblk, yblk, yblk, fblk, fblk, pblk]
    args = [f, *rims, potential]
    if last:
        in_specs.append(blk)
        args.append(orbitals)
        out_specs = blk
        out_shape = jax.ShapeDtypeStruct(f.shape, jnp.float32)
    else:
        out_specs = (blk, fblk)
        out_shape = (jax.ShapeDtypeStruct(f.shape, jnp.float32),
                     jax.ShapeDtypeStruct((norb, 8, cx * cy), jnp.float32))
    return pl.pallas_call(
        functools.partial(stage_kernel, last=last), grid=(norb // BLOCK,), in_specs=in_specs,
        out_specs=out_specs, out_shape=out_shape, interpret=INTERPRET,
        compiler_params=pltpu.CompilerParams(dimension_semantics=("arbitrary",)),
    )(*args)


def solve_kernel(l_ref, y_ref, o_ref):
    n = y_ref.shape[0]
    for j in range(n):
        acc = y_ref[j]
        for k in range(j):
            acc = acc - l_ref[j, k] * o_ref[k]
        o_ref[j] = acc / l_ref[j, j]


def solve_lower(lower, y):
    norb, cx, cy, cz = y.shape
    xb = 2
    blk = pl.BlockSpec((norb, xb, cy, cz), lambda i: (0, i, 0, 0))
    return pl.pallas_call(
        solve_kernel, grid=(cx // xb,),
        in_specs=[pl.BlockSpec(memory_space=pltpu.SMEM), blk], out_specs=blk,
        out_shape=jax.ShapeDtypeStruct(y.shape, jnp.float32), interpret=INTERPRET,
    )(lower, y)


def butterfly_sum(c):
    for axis in ("gz", "gy", "gx"):
        n = lax.axis_size(axis)
        d = 1
        while d < n:
            c = c + lax.ppermute(c, axis, [(i, i ^ d) for i in range(n)])
            d *= 2
    return c


def per_device(orbitals, potential):
    first, first_z = stage(orbitals, exchange(orbitals, z_faces(orbitals)), potential)
    second = stage(first, exchange(first, first_z), potential, orbitals)
    norb_count = orbitals.shape[0]
    all_cells = second[0].size * lax.axis_size("gx") * lax.axis_size("gy") * lax.axis_size("gz")
    correlation = jnp.einsum("axyz,bxyz->ab", second, second, precision=HI) / all_cells
    lower = jnp.linalg.cholesky(butterfly_sum(correlation))
    basis = solve_lower(lower, second)
    return (basis, lower.T)


def solution(mesh):
    in_specs = (P(None, "gx", "gy", "gz"), P("gx", "gy", "gz"))
    out_specs = (P(None, "gx", "gy", "gz"), P())
    return jax.shard_map(
        per_device, mesh=mesh, in_specs=in_specs, out_specs=out_specs, check_vma=False
    )
```

```python
import functools

import jax
import jax.numpy as jnp
from jax import lax
from jax.experimental import pallas as pl
from jax.experimental.pallas import tpu as pltpu
from jax.sharding import PartitionSpec as P

TAPS = (-1.0 / 12.0, 4.0 / 3.0, -2.5, 4.0 / 3.0, -1.0 / 12.0)
BLOCK = 8
INTERPRET = False
HI = lax.Precision.HIGHEST


def shift_pairs(n, step):
    return [(i, (i + step) % n) for i in range(n)]


def face_lanes(plane, orbital, lane, packed):
    cz = plane.shape[1]
    rolled = pltpu.roll(plane, (4 * orbital + 2) % cz, 1)
    return jnp.where(lane // 4 == orbital, rolled, packed)


def stage_kernel(*refs, last):
    if last:
        (f_ref, xlo_ref, xhi_ref, ylo_ref, yhi_ref, zlo_ref, zhi_ref, pot_ref, orb_ref,
         out_ref) = refs
    else:
        (f_ref, xlo_ref, xhi_ref, ylo_ref, yhi_ref, zlo_ref, zhi_ref, pot_ref,
         out_ref, face_ref) = refs
    nb, cx, cy, cz = f_ref.shape
    rows = cx * cy
    step = pl.program_id(0)
    lane = lax.broadcasted_iota(jnp.int32, (rows, cz), 1)
    yid = lax.broadcasted_iota(jnp.int32, (cx, cy, cz), 1)
    pot = pot_ref[...]
    zlo = zlo_ref[...]
    zhi = zhi_ref[...]
    if not last:
        @pl.when(step == 0)
        def _():
            face_ref[...] = jnp.zeros(face_ref.shape, jnp.float32)
        packed = face_ref[...]
    for b in range(nb):
        orbital = step * nb + b
        f3 = f_ref[b]
        summed = 3.0 * TAPS[2] * f3
        ext = jnp.concatenate([xlo_ref[b], f3, xhi_ref[b]], axis=0)
        for offset, weight in ((-2, TAPS[0]), (-1, TAPS[1]), (1, TAPS[3]), (2, TAPS[4])):
            summed = summed + weight * ext[2 + offset: 2 + offset + cx]
        ylo = ylo_ref[b]
        yhi = yhi_ref[b]
        ym2 = jnp.where(yid == 0, ylo[:, 0:1, :], jnp.where(yid == 1, ylo[:, 1:2, :], pltpu.roll(f3, 2, 1)))
        ym1 = jnp.where(yid == 0, ylo[:, 1:2, :], pltpu.roll(f3, 1, 1))
        yp1 = jnp.where(yid == cy - 1, yhi[:, 0:1, :], pltpu.roll(f3, cy - 1, 1))
        yp2 = jnp.where(yid == cy - 2, yhi[:, 0:1, :], jnp.where(yid == cy - 1, yhi[:, 1:2, :], pltpu.roll(f3, cy - 2, 1)))
        for shifted, weight in ((ym2, TAPS[0]), (ym1, TAPS[1]), (yp1, TAPS[3]), (yp2, TAPS[4])):
            summed = summed + weight * shifted
        f2 = f3.reshape(rows, cz)
        base = 4 * orbital
        zm2 = jnp.where(lane < 2, pltpu.roll(zlo, (cz - base) % cz, 1), pltpu.roll(f2, 2, 1))
        zm1 = jnp.where(lane < 1, pltpu.roll(zlo, cz - 1 - base, 1), pltpu.roll(f2, 1, 1))
        zp1 = jnp.where(lane >= cz - 1, pltpu.roll(zhi, cz - 3 - base, 1), pltpu.roll(f2, cz - 1, 1))
        zp2 = jnp.where(lane >= cz - 2, pltpu.roll(zhi, cz - 4 - base, 1), pltpu.roll(f2, cz - 2, 1))
        summed = summed.reshape(rows, cz)
        for shifted, weight in ((zm2, TAPS[0]), (zm1, TAPS[1]), (zp1, TAPS[3]), (zp2, TAPS[4])):
            summed = summed + weight * shifted
        pot2 = pot.reshape(rows, cz)
        h = -0.5 * summed + pot2 * f2
        if last:
            res = 2.0 * (h - 5.5 * f2) / 3.5 - orb_ref[b].reshape(rows, cz)
        else:
            res = (h - 5.5 * f2) / 3.5
            packed = face_lanes(res, orbital, lane, packed)
        out_ref[b] = res.reshape(cx, cy, cz)
    if not last:
        face_ref[...] = packed


def z_face_kernel(f_ref, face_ref):
    nb, cx, cy, cz = f_ref.shape
    step = pl.program_id(0)
    lane = lax.broadcasted_iota(jnp.int32, (cx * cy, cz), 1)

    @pl.when(step == 0)
    def _():
        face_ref[...] = jnp.zeros(face_ref.shape, jnp.float32)

    packed = face_ref[...]
    for b in range(nb):
        packed = face_lanes(f_ref[b].reshape(cx * cy, cz), step * nb + b, lane, packed)
    face_ref[...] = packed


def z_faces(f):
    norb, cx, cy, cz = f.shape
    blk = pl.BlockSpec((BLOCK, cx, cy, cz), lambda i: (i, 0, 0, 0))
    fblk = pl.BlockSpec((cx * cy, 4 * norb), lambda i: (0, 0))
    return pl.pallas_call(
        z_face_kernel, grid=(norb // BLOCK,), in_specs=[blk], out_specs=fblk,
        out_shape=jax.ShapeDtypeStruct((cx * cy, 4 * norb), jnp.float32), interpret=INTERPRET,
        compiler_params=pltpu.CompilerParams(dimension_semantics=("arbitrary",)),
    )(f)


def exchange(f, zface):
    out = []
    for axis, dim in (("gx", 1), ("gy", 2)):
        n, length = lax.axis_size(axis), f.shape[dim]
        last = lax.slice_in_dim(f, length - 2, length, axis=dim)
        first = lax.slice_in_dim(f, 0, 2, axis=dim)
        out.append(lax.ppermute(last, axis, shift_pairs(n, 1)))
        out.append(lax.ppermute(first, axis, shift_pairs(n, -1)))
    n = lax.axis_size("gz")
    out.append(lax.ppermute(zface, "gz", shift_pairs(n, 1)))
    out.append(lax.ppermute(zface, "gz", shift_pairs(n, -1)))
    return out


def stage(f, rims, potential, orbitals=None):
    norb, cx, cy, cz = f.shape
    last = orbitals is not None
    blk = pl.BlockSpec((BLOCK, cx, cy, cz), lambda i: (i, 0, 0, 0))
    xblk = pl.BlockSpec((BLOCK, 2, cy, cz), lambda i: (i, 0, 0, 0))
    yblk = pl.BlockSpec((BLOCK, cx, 2, cz), lambda i: (i, 0, 0, 0))
    fblk = pl.BlockSpec((cx * cy, 4 * norb), lambda i: (0, 0))
    pblk = pl.BlockSpec((cx, cy, cz), lambda i: (0, 0, 0))
    in_specs = [blk, xblk, xblk, yblk, yblk, fblk, fblk, pblk]
    args = [f, *rims, potential]
    if last:
        in_specs.append(blk)
        args.append(orbitals)
        out_specs = blk
        out_shape = jax.ShapeDtypeStruct(f.shape, jnp.float32)
    else:
        out_specs = (blk, fblk)
        out_shape = (jax.ShapeDtypeStruct(f.shape, jnp.float32),
                     jax.ShapeDtypeStruct((cx * cy, 4 * norb), jnp.float32))
    return pl.pallas_call(
        functools.partial(stage_kernel, last=last), grid=(norb // BLOCK,), in_specs=in_specs,
        out_specs=out_specs, out_shape=out_shape, interpret=INTERPRET,
        compiler_params=pltpu.CompilerParams(dimension_semantics=("arbitrary",)),
    )(*args)


def solve_kernel(l_ref, y_ref, o_ref):
    n = y_ref.shape[0]
    for j in range(n):
        acc = y_ref[j]
        for k in range(j):
            acc = acc - l_ref[j, k] * o_ref[k]
        o_ref[j] = acc / l_ref[j, j]


def solve_lower(lower, y):
    norb, cx, cy, cz = y.shape
    xb = 2
    blk = pl.BlockSpec((norb, xb, cy, cz), lambda i: (0, i, 0, 0))
    return pl.pallas_call(
        solve_kernel, grid=(cx // xb,),
        in_specs=[pl.BlockSpec(memory_space=pltpu.SMEM), blk], out_specs=blk,
        out_shape=jax.ShapeDtypeStruct(y.shape, jnp.float32), interpret=INTERPRET,
    )(lower, y)


def butterfly_sum(c):
    for axis in ("gz", "gy", "gx"):
        n = lax.axis_size(axis)
        d = 1
        while d < n:
            c = c + lax.ppermute(c, axis, [(i, i ^ d) for i in range(n)])
            d *= 2
    return c


def per_device(orbitals, potential):
    first, first_z = stage(orbitals, exchange(orbitals, z_faces(orbitals)), potential)
    second = stage(first, exchange(first, first_z), potential, orbitals)
    norb_count = orbitals.shape[0]
    all_cells = second[0].size * lax.axis_size("gx") * lax.axis_size("gy") * lax.axis_size("gz")
    correlation = jnp.einsum("axyz,bxyz->ab", second, second, precision=HI) / all_cells
    lower = jnp.linalg.cholesky(butterfly_sum(correlation))
    basis = solve_lower(lower, second)
    return (basis, lower.T)


def solution(mesh):
    in_specs = (P(None, "gx", "gy", "gz"), P("gx", "gy", "gz"))
    out_specs = (P(None, "gx", "gy", "gz"), P())
    return jax.shard_map(
        per_device, mesh=mesh, in_specs=in_specs, out_specs=out_specs, check_vma=False
    )
```

```python
import functools

import jax
import jax.numpy as jnp
from jax import lax
from jax.experimental import pallas as pl
from jax.experimental.pallas import tpu as pltpu
from jax.sharding import PartitionSpec as P

TAPS = (-1.0 / 12.0, 4.0 / 3.0, -2.5, 4.0 / 3.0, -1.0 / 12.0)
BLOCK = 8
INTERPRET = False
HI = lax.Precision.HIGHEST


def shift_pairs(n, step):
    return [(i, (i + step) % n) for i in range(n)]


def face_lanes(plane, orbital, lane, packed):
    cz = plane.shape[1]
    rolled = pltpu.roll(plane, (4 * orbital + 2) % cz, 1)
    return jnp.where(lane // 4 == orbital, rolled, packed)


def stage_kernel(*refs, last):
    if last:
        (f_ref, xlo_ref, xhi_ref, ylo_ref, yhi_ref, zlo_ref, zhi_ref, pot_ref, orb_ref,
         out_ref) = refs
    else:
        (f_ref, xlo_ref, xhi_ref, ylo_ref, yhi_ref, zlo_ref, zhi_ref, pot_ref,
         out_ref, face_ref) = refs
    nb, cx, cy, cz = f_ref.shape
    rows = cx * cy
    step = pl.program_id(0)
    lane = lax.broadcasted_iota(jnp.int32, (rows, cz), 1)
    yid = lax.broadcasted_iota(jnp.int32, (cx, cy, cz), 1)
    pot = pot_ref[...]
    zlo = zlo_ref[...]
    zhi = zhi_ref[...]
    if not last:
        @pl.when(step == 0)
        def _():
            face_ref[...] = jnp.zeros(face_ref.shape, jnp.float32)
        packed = face_ref[...]
    for b in range(nb):
        orbital = step * nb + b
        f3 = f_ref[b]
        summed = 3.0 * TAPS[2] * f3
        ext = jnp.concatenate([xlo_ref[b], f3, xhi_ref[b]], axis=0)
        for offset, weight in ((-2, TAPS[0]), (-1, TAPS[1]), (1, TAPS[3]), (2, TAPS[4])):
            summed = summed + weight * ext[2 + offset: 2 + offset + cx]
        ylo = ylo_ref[b]
        yhi = yhi_ref[b]
        ym2 = jnp.where(yid == 0, ylo[:, 0:1, :], jnp.where(yid == 1, ylo[:, 1:2, :], pltpu.roll(f3, 2, 1)))
        ym1 = jnp.where(yid == 0, ylo[:, 1:2, :], pltpu.roll(f3, 1, 1))
        yp1 = jnp.where(yid == cy - 1, yhi[:, 0:1, :], pltpu.roll(f3, cy - 1, 1))
        yp2 = jnp.where(yid == cy - 2, yhi[:, 0:1, :], jnp.where(yid == cy - 1, yhi[:, 1:2, :], pltpu.roll(f3, cy - 2, 1)))
        for shifted, weight in ((ym2, TAPS[0]), (ym1, TAPS[1]), (yp1, TAPS[3]), (yp2, TAPS[4])):
            summed = summed + weight * shifted
        f2 = f3.reshape(rows, cz)
        base = 4 * orbital
        zm2 = jnp.where(lane < 2, pltpu.roll(zlo, (cz - base) % cz, 1), pltpu.roll(f2, 2, 1))
        zm1 = jnp.where(lane < 1, pltpu.roll(zlo, cz - 1 - base, 1), pltpu.roll(f2, 1, 1))
        zp1 = jnp.where(lane >= cz - 1, pltpu.roll(zhi, cz - 3 - base, 1), pltpu.roll(f2, cz - 1, 1))
        zp2 = jnp.where(lane >= cz - 2, pltpu.roll(zhi, cz - 4 - base, 1), pltpu.roll(f2, cz - 2, 1))
        summed = summed.reshape(rows, cz)
        for shifted, weight in ((zm2, TAPS[0]), (zm1, TAPS[1]), (zp1, TAPS[3]), (zp2, TAPS[4])):
            summed = summed + weight * shifted
        pot2 = pot.reshape(rows, cz)
        h = -0.5 * summed + pot2 * f2
        if last:
            res = 2.0 * (h - 5.5 * f2) / 3.5 - orb_ref[b].reshape(rows, cz)
        else:
            res = (h - 5.5 * f2) / 3.5
            packed = face_lanes(res, orbital, lane, packed)
        out_ref[b] = res.reshape(cx, cy, cz)
    if not last:
        face_ref[...] = packed


def z_face_kernel(f_ref, face_ref):
    nb, cx, cy, cz = f_ref.shape
    step = pl.program_id(0)
    lane = lax.broadcasted_iota(jnp.int32, (cx * cy, cz), 1)

    @pl.when(step == 0)
    def _():
        face_ref[...] = jnp.zeros(face_ref.shape, jnp.float32)

    packed = face_ref[...]
    for b in range(nb):
        packed = face_lanes(f_ref[b].reshape(cx * cy, cz), step * nb + b, lane, packed)
    face_ref[...] = packed


def z_faces(f):
    norb, cx, cy, cz = f.shape
    blk = pl.BlockSpec((BLOCK, cx, cy, cz), lambda i: (i, 0, 0, 0))
    fblk = pl.BlockSpec((cx * cy, 4 * norb), lambda i: (0, 0))
    return pl.pallas_call(
        z_face_kernel, grid=(norb // BLOCK,), in_specs=[blk], out_specs=fblk,
        out_shape=jax.ShapeDtypeStruct((cx * cy, 4 * norb), jnp.float32), interpret=INTERPRET,
        compiler_params=pltpu.CompilerParams(dimension_semantics=("arbitrary",)),
    )(f)


def exchange(f, zface):
    out = []
    for axis, dim in (("gx", 1), ("gy", 2)):
        n, length = lax.axis_size(axis), f.shape[dim]
        last = lax.slice_in_dim(f, length - 2, length, axis=dim)
        first = lax.slice_in_dim(f, 0, 2, axis=dim)
        out.append(lax.ppermute(last, axis, shift_pairs(n, 1)))
        out.append(lax.ppermute(first, axis, shift_pairs(n, -1)))
    n = lax.axis_size("gz")
    out.append(lax.ppermute(zface, "gz", shift_pairs(n, 1)))
    out.append(lax.ppermute(zface, "gz", shift_pairs(n, -1)))
    return out


def stage(f, rims, potential, orbitals=None):
    norb, cx, cy, cz = f.shape
    last = orbitals is not None
    blk = pl.BlockSpec((BLOCK, cx, cy, cz), lambda i: (i, 0, 0, 0))
    xblk = pl.BlockSpec((BLOCK, 2, cy, cz), lambda i: (i, 0, 0, 0))
    yblk = pl.BlockSpec((BLOCK, cx, 2, cz), lambda i: (i, 0, 0, 0))
    fblk = pl.BlockSpec((cx * cy, 4 * norb), lambda i: (0, 0))
    pblk = pl.BlockSpec((cx, cy, cz), lambda i: (0, 0, 0))
    in_specs = [blk, xblk, xblk, yblk, yblk, fblk, fblk, pblk]
    args = [f, *rims, potential]
    if last:
        in_specs.append(blk)
        args.append(orbitals)
        out_specs = blk
        out_shape = jax.ShapeDtypeStruct(f.shape, jnp.float32)
    else:
        out_specs = (blk, fblk)
        out_shape = (jax.ShapeDtypeStruct(f.shape, jnp.float32),
                     jax.ShapeDtypeStruct((cx * cy, 4 * norb), jnp.float32))
    return pl.pallas_call(
        functools.partial(stage_kernel, last=last), grid=(norb // BLOCK,), in_specs=in_specs,
        out_specs=out_specs, out_shape=out_shape, interpret=INTERPRET,
        compiler_params=pltpu.CompilerParams(dimension_semantics=("arbitrary",)),
    )(*args)


def solve_kernel(l_ref, y_ref, o_ref):
    n = y_ref.shape[0]
    for j in range(n):
        acc = y_ref[j]
        other = None
        for k in range(j):
            term = l_ref[j, k] * o_ref[k]
            if k % 2 == 0:
                acc = acc - term
            else:
                other = term if other is None else other + term
        if other is not None:
            acc = acc - other
        o_ref[j] = acc / l_ref[j, j]


def solve_lower(lower, y):
    norb, cx, cy, cz = y.shape
    xb = 4
    blk = pl.BlockSpec((norb, xb, cy, cz), lambda i: (0, i, 0, 0))
    return pl.pallas_call(
        solve_kernel, grid=(cx // xb,),
        in_specs=[pl.BlockSpec(memory_space=pltpu.SMEM), blk], out_specs=blk,
        out_shape=jax.ShapeDtypeStruct(y.shape, jnp.float32), interpret=INTERPRET,
    )(lower, y)


def butterfly_sum(c):
    for axis in ("gz", "gy", "gx"):
        n = lax.axis_size(axis)
        d = 1
        while d < n:
            c = c + lax.ppermute(c, axis, [(i, i ^ d) for i in range(n)])
            d *= 2
    return c


def per_device(orbitals, potential):
    first, first_z = stage(orbitals, exchange(orbitals, z_faces(orbitals)), potential)
    second = stage(first, exchange(first, first_z), potential, orbitals)
    norb_count = orbitals.shape[0]
    all_cells = second[0].size * lax.axis_size("gx") * lax.axis_size("gy") * lax.axis_size("gz")
    correlation = jnp.einsum("axyz,bxyz->ab", second, second, precision=HI) / all_cells
    lower = jnp.linalg.cholesky(butterfly_sum(correlation))
    basis = solve_lower(lower, second)
    return (basis, lower.T)


def solution(mesh):
    in_specs = (P(None, "gx", "gy", "gz"), P("gx", "gy", "gz"))
    out_specs = (P(None, "gx", "gy", "gz"), P())
    return jax.shard_map(
        per_device, mesh=mesh, in_specs=in_specs, out_specs=out_specs, check_vma=False
    )
```

```python
import functools

import jax
import jax.numpy as jnp
from jax import lax
from jax.experimental import pallas as pl
from jax.experimental.pallas import tpu as pltpu
from jax.sharding import PartitionSpec as P

TAPS = (-1.0 / 12.0, 4.0 / 3.0, -2.5, 4.0 / 3.0, -1.0 / 12.0)
BLOCK = 8
INTERPRET = False
HI = lax.Precision.HIGHEST


def shift_pairs(n, step):
    return [(i, (i + step) % n) for i in range(n)]


def face_lanes(plane, orbital, lane, packed):
    cz = plane.shape[1]
    rolled = pltpu.roll(plane, (4 * orbital + 2) % cz, 1)
    return jnp.where(lane // 4 == orbital, rolled, packed)


def stage_kernel(*refs, last):
    if last:
        (f_ref, xlo_ref, xhi_ref, ylo_ref, yhi_ref, zlo_ref, zhi_ref, pot_ref, orb_ref,
         out_ref) = refs
    else:
        (f_ref, xlo_ref, xhi_ref, ylo_ref, yhi_ref, zlo_ref, zhi_ref, pot_ref,
         out_ref, face_ref) = refs
    nb, cx, cy, cz = f_ref.shape
    rows = cx * cy
    step = pl.program_id(0)
    lane = lax.broadcasted_iota(jnp.int32, (rows, cz), 1)
    yid = lax.broadcasted_iota(jnp.int32, (cx, cy, cz), 1)
    pot = pot_ref[...]
    zlo = zlo_ref[...]
    zhi = zhi_ref[...]
    if not last:
        @pl.when(step == 0)
        def _():
            face_ref[...] = jnp.zeros(face_ref.shape, jnp.float32)
        packed = face_ref[...]
    for b in range(nb):
        orbital = step * nb + b
        f3 = f_ref[b]
        summed = 3.0 * TAPS[2] * f3
        ext = jnp.concatenate([xlo_ref[b], f3, xhi_ref[b]], axis=0)
        for offset, weight in ((-2, TAPS[0]), (-1, TAPS[1]), (1, TAPS[3]), (2, TAPS[4])):
            summed = summed + weight * ext[2 + offset: 2 + offset + cx]
        ylo = ylo_ref[b]
        yhi = yhi_ref[b]
        ym2 = jnp.where(yid == 0, ylo[:, 0:1, :], jnp.where(yid == 1, ylo[:, 1:2, :], pltpu.roll(f3, 2, 1)))
        ym1 = jnp.where(yid == 0, ylo[:, 1:2, :], pltpu.roll(f3, 1, 1))
        yp1 = jnp.where(yid == cy - 1, yhi[:, 0:1, :], pltpu.roll(f3, cy - 1, 1))
        yp2 = jnp.where(yid == cy - 2, yhi[:, 0:1, :], jnp.where(yid == cy - 1, yhi[:, 1:2, :], pltpu.roll(f3, cy - 2, 1)))
        for shifted, weight in ((ym2, TAPS[0]), (ym1, TAPS[1]), (yp1, TAPS[3]), (yp2, TAPS[4])):
            summed = summed + weight * shifted
        f2 = f3.reshape(rows, cz)
        base = 4 * orbital
        zm2 = jnp.where(lane < 2, pltpu.roll(zlo, (cz - base) % cz, 1), pltpu.roll(f2, 2, 1))
        zm1 = jnp.where(lane < 1, pltpu.roll(zlo, cz - 1 - base, 1), pltpu.roll(f2, 1, 1))
        zp1 = jnp.where(lane >= cz - 1, pltpu.roll(zhi, cz - 3 - base, 1), pltpu.roll(f2, cz - 1, 1))
        zp2 = jnp.where(lane >= cz - 2, pltpu.roll(zhi, cz - 4 - base, 1), pltpu.roll(f2, cz - 2, 1))
        summed = summed.reshape(rows, cz)
        for shifted, weight in ((zm2, TAPS[0]), (zm1, TAPS[1]), (zp1, TAPS[3]), (zp2, TAPS[4])):
            summed = summed + weight * shifted
        pot2 = pot.reshape(rows, cz)
        h = -0.5 * summed + pot2 * f2
        if last:
            res = 2.0 * (h - 5.5 * f2) / 3.5 - orb_ref[b].reshape(rows, cz)
        else:
            res = (h - 5.5 * f2) / 3.5
            packed = face_lanes(res, orbital, lane, packed)
        out_ref[b] = res.reshape(cx, cy, cz)
    if not last:
        face_ref[...] = packed


def z_face_kernel(f_ref, face_ref):
    nb, cx, cy, cz = f_ref.shape
    step = pl.program_id(0)
    lane = lax.broadcasted_iota(jnp.int32, (cx * cy, cz), 1)

    @pl.when(step == 0)
    def _():
        face_ref[...] = jnp.zeros(face_ref.shape, jnp.float32)

    packed = face_ref[...]
    for b in range(nb):
        packed = face_lanes(f_ref[b].reshape(cx * cy, cz), step * nb + b, lane, packed)
    face_ref[...] = packed


def z_faces(f):
    norb, cx, cy, cz = f.shape
    blk = pl.BlockSpec((BLOCK, cx, cy, cz), lambda i: (i, 0, 0, 0))
    fblk = pl.BlockSpec((cx * cy, 4 * norb), lambda i: (0, 0))
    return pl.pallas_call(
        z_face_kernel, grid=(norb // BLOCK,), in_specs=[blk], out_specs=fblk,
        out_shape=jax.ShapeDtypeStruct((cx * cy, 4 * norb), jnp.float32), interpret=INTERPRET,
        compiler_params=pltpu.CompilerParams(dimension_semantics=("arbitrary",)),
    )(f)


def exchange(f, zface):
    out = []
    for axis, dim in (("gx", 1), ("gy", 2)):
        n, length = lax.axis_size(axis), f.shape[dim]
        last = lax.slice_in_dim(f, length - 2, length, axis=dim)
        first = lax.slice_in_dim(f, 0, 2, axis=dim)
        out.append(lax.ppermute(last, axis, shift_pairs(n, 1)))
        out.append(lax.ppermute(first, axis, shift_pairs(n, -1)))
    n = lax.axis_size("gz")
    out.append(lax.ppermute(zface, "gz", shift_pairs(n, 1)))
    out.append(lax.ppermute(zface, "gz", shift_pairs(n, -1)))
    return out


def stage(f, rims, potential, orbitals=None):
    norb, cx, cy, cz = f.shape
    last = orbitals is not None
    blk = pl.BlockSpec((BLOCK, cx, cy, cz), lambda i: (i, 0, 0, 0))
    xblk = pl.BlockSpec((BLOCK, 2, cy, cz), lambda i: (i, 0, 0, 0))
    yblk = pl.BlockSpec((BLOCK, cx, 2, cz), lambda i: (i, 0, 0, 0))
    fblk = pl.BlockSpec((cx * cy, 4 * norb), lambda i: (0, 0))
    pblk = pl.BlockSpec((cx, cy, cz), lambda i: (0, 0, 0))
    in_specs = [blk, xblk, xblk, yblk, yblk, fblk, fblk, pblk]
    args = [f, *rims, potential]
    if last:
        in_specs.append(blk)
        args.append(orbitals)
        out_specs = blk
        out_shape = jax.ShapeDtypeStruct(f.shape, jnp.float32)
    else:
        out_specs = (blk, fblk)
        out_shape = (jax.ShapeDtypeStruct(f.shape, jnp.float32),
                     jax.ShapeDtypeStruct((cx * cy, 4 * norb), jnp.float32))
    return pl.pallas_call(
        functools.partial(stage_kernel, last=last), grid=(norb // BLOCK,), in_specs=in_specs,
        out_specs=out_specs, out_shape=out_shape, interpret=INTERPRET,
        compiler_params=pltpu.CompilerParams(dimension_semantics=("arbitrary",)),
    )(*args)


def solve_kernel(l_ref, y_ref, o_ref):
    n = y_ref.shape[0]
    for j in range(n):
        acc = y_ref[j]
        other = None
        for k in range(j):
            term = l_ref[j, k] * o_ref[k]
            if k % 2 == 0:
                acc = acc - term
            else:
                other = term if other is None else other + term
        if other is not None:
            acc = acc - other
        o_ref[j] = acc / l_ref[j, j]


def solve_lower(lower, y):
    norb, cx, cy, cz = y.shape
    xb = 4
    blk = pl.BlockSpec((norb, xb, cy, cz), lambda i: (0, i, 0, 0))
    return pl.pallas_call(
        solve_kernel, grid=(cx // xb,),
        in_specs=[pl.BlockSpec(memory_space=pltpu.SMEM), blk], out_specs=blk,
        out_shape=jax.ShapeDtypeStruct(y.shape, jnp.float32), interpret=INTERPRET,
    )(lower, y)


def gram_kernel(y_ref, o_ref, acc_ref):
    n, xb, cy, cz = y_ref.shape
    step = pl.program_id(0)

    @pl.when(step == 0)
    def _():
        acc_ref[...] = jnp.zeros(acc_ref.shape, jnp.float32)

    idx = 0
    for a in range(n):
        ya = y_ref[a].reshape(xb * cy // 8, 8, cz)
        for b in range(a, n):
            yb = y_ref[b].reshape(xb * cy // 8, 8, cz)
            acc_ref[idx] += (ya * yb).sum(axis=0)
            idx += 1

    @pl.when(step == pl.num_programs(0) - 1)
    def _():
        idx = 0
        for a in range(n):
            for b in range(a, n):
                row = jnp.sum(acc_ref[idx], axis=0, keepdims=True)
                o_ref[pl.ds(a * n + b, 1), :] = row
                if b != a:
                    o_ref[pl.ds(b * n + a, 1), :] = row
                idx += 1


def gram(y):
    norb, cx, cy, cz = y.shape
    xb = 4
    pairs = norb * (norb + 1) // 2
    lanes = pl.pallas_call(
        gram_kernel, grid=(cx // xb,),
        in_specs=[pl.BlockSpec((norb, xb, cy, cz), lambda i: (0, i, 0, 0))],
        out_specs=pl.BlockSpec((norb * norb, cz), lambda i: (0, 0)),
        out_shape=jax.ShapeDtypeStruct((norb * norb, cz), jnp.float32),
        scratch_shapes=[pltpu.VMEM((pairs, 8, cz), jnp.float32)], interpret=INTERPRET,
        compiler_params=pltpu.CompilerParams(dimension_semantics=("arbitrary",)),
    )(y)
    return lanes.sum(axis=1).reshape(norb, norb)


def butterfly_sum(c):
    for axis in ("gz", "gy", "gx"):
        n = lax.axis_size(axis)
        d = 1
        while d < n:
            c = c + lax.ppermute(c, axis, [(i, i ^ d) for i in range(n)])
            d *= 2
    return c


def per_device(orbitals, potential):
    first, first_z = stage(orbitals, exchange(orbitals, z_faces(orbitals)), potential)
    second = stage(first, exchange(first, first_z), potential, orbitals)
    norb_count = orbitals.shape[0]
    all_cells = second[0].size * lax.axis_size("gx") * lax.axis_size("gy") * lax.axis_size("gz")
    correlation = gram(second) / all_cells
    lower = jnp.linalg.cholesky(butterfly_sum(correlation))
    basis = solve_lower(lower, second)
    return (basis, lower.T)


def solution(mesh):
    in_specs = (P(None, "gx", "gy", "gz"), P("gx", "gy", "gz"))
    out_specs = (P(None, "gx", "gy", "gz"), P())
    return jax.shard_map(
        per_device, mesh=mesh, in_specs=in_specs, out_specs=out_specs, check_vma=False
    )
```

```python
import functools

import jax
import jax.numpy as jnp
from jax import lax
from jax.experimental import pallas as pl
from jax.experimental.pallas import tpu as pltpu
from jax.sharding import PartitionSpec as P

TAPS = (-1.0 / 12.0, 4.0 / 3.0, -2.5, 4.0 / 3.0, -1.0 / 12.0)
BLOCK = 8
INTERPRET = False
HI = lax.Precision.HIGHEST


def shift_pairs(n, step):
    return [(i, (i + step) % n) for i in range(n)]


def face_lanes(plane, orbital, lane, packed):
    cz = plane.shape[1]
    rolled = pltpu.roll(plane, (4 * orbital + 2) % cz, 1)
    return jnp.where(lane // 4 == orbital, rolled, packed)


def stage_kernel(*refs, last):
    if last:
        (f_ref, xlo_ref, xhi_ref, ylo_ref, yhi_ref, zlo_ref, zhi_ref, pot_ref, orb_ref,
         out_ref) = refs
    else:
        (f_ref, xlo_ref, xhi_ref, ylo_ref, yhi_ref, zlo_ref, zhi_ref, pot_ref,
         out_ref, face_ref, xl_ref, xf_ref, yl_ref, yf_ref) = refs
    nb, cx, cy, cz = f_ref.shape
    rows = cx * cy
    step = pl.program_id(0)
    lane = lax.broadcasted_iota(jnp.int32, (rows, cz), 1)
    yid = lax.broadcasted_iota(jnp.int32, (cx, cy, cz), 1)
    pot = pot_ref[...]
    zlo = zlo_ref[...]
    zhi = zhi_ref[...]
    if not last:
        @pl.when(step == 0)
        def _():
            face_ref[...] = jnp.zeros(face_ref.shape, jnp.float32)
        packed = face_ref[...]
    for b in range(nb):
        orbital = step * nb + b
        f3 = f_ref[b]
        summed = 3.0 * TAPS[2] * f3
        ext = jnp.concatenate([xlo_ref[b], f3, xhi_ref[b]], axis=0)
        for offset, weight in ((-2, TAPS[0]), (-1, TAPS[1]), (1, TAPS[3]), (2, TAPS[4])):
            summed = summed + weight * ext[2 + offset: 2 + offset + cx]
        ylo = ylo_ref[b]
        yhi = yhi_ref[b]
        ym2 = jnp.where(yid == 0, ylo[:, 0:1, :], jnp.where(yid == 1, ylo[:, 1:2, :], pltpu.roll(f3, 2, 1)))
        ym1 = jnp.where(yid == 0, ylo[:, 1:2, :], pltpu.roll(f3, 1, 1))
        yp1 = jnp.where(yid == cy - 1, yhi[:, 0:1, :], pltpu.roll(f3, cy - 1, 1))
        yp2 = jnp.where(yid == cy - 2, yhi[:, 0:1, :], jnp.where(yid == cy - 1, yhi[:, 1:2, :], pltpu.roll(f3, cy - 2, 1)))
        for shifted, weight in ((ym2, TAPS[0]), (ym1, TAPS[1]), (yp1, TAPS[3]), (yp2, TAPS[4])):
            summed = summed + weight * shifted
        f2 = f3.reshape(rows, cz)
        base = 4 * orbital
        zm2 = jnp.where(lane < 2, pltpu.roll(zlo, (cz - base) % cz, 1), pltpu.roll(f2, 2, 1))
        zm1 = jnp.where(lane < 1, pltpu.roll(zlo, cz - 1 - base, 1), pltpu.roll(f2, 1, 1))
        zp1 = jnp.where(lane >= cz - 1, pltpu.roll(zhi, cz - 3 - base, 1), pltpu.roll(f2, cz - 1, 1))
        zp2 = jnp.where(lane >= cz - 2, pltpu.roll(zhi, cz - 4 - base, 1), pltpu.roll(f2, cz - 2, 1))
        summed = summed.reshape(rows, cz)
        for shifted, weight in ((zm2, TAPS[0]), (zm1, TAPS[1]), (zp1, TAPS[3]), (zp2, TAPS[4])):
            summed = summed + weight * shifted
        pot2 = pot.reshape(rows, cz)
        h = -0.5 * summed + pot2 * f2
        if last:
            res = 2.0 * (h - 5.5 * f2) / 3.5 - orb_ref[b].reshape(rows, cz)
        else:
            res = (h - 5.5 * f2) / 3.5
            packed = face_lanes(res, orbital, lane, packed)
        res3 = res.reshape(cx, cy, cz)
        out_ref[b] = res3
        if not last:
            xl_ref[b] = res3[cx - 2:]
            xf_ref[b] = res3[:2]
            yl_ref[b] = res3[:, cy - 2:, :]
            yf_ref[b] = res3[:, :2, :]
    if not last:
        face_ref[...] = packed


def z_face_kernel(f_ref, face_ref):
    nb, cx, cy, cz = f_ref.shape
    step = pl.program_id(0)
    lane = lax.broadcasted_iota(jnp.int32, (cx * cy, cz), 1)

    @pl.when(step == 0)
    def _():
        face_ref[...] = jnp.zeros(face_ref.shape, jnp.float32)

    packed = face_ref[...]
    for b in range(nb):
        packed = face_lanes(f_ref[b].reshape(cx * cy, cz), step * nb + b, lane, packed)
    face_ref[...] = packed


def z_faces(f):
    norb, cx, cy, cz = f.shape
    blk = pl.BlockSpec((BLOCK, cx, cy, cz), lambda i: (i, 0, 0, 0))
    fblk = pl.BlockSpec((cx * cy, 4 * norb), lambda i: (0, 0))
    return pl.pallas_call(
        z_face_kernel, grid=(norb // BLOCK,), in_specs=[blk], out_specs=fblk,
        out_shape=jax.ShapeDtypeStruct((cx * cy, 4 * norb), jnp.float32), interpret=INTERPRET,
        compiler_params=pltpu.CompilerParams(dimension_semantics=("arbitrary",)),
    )(f)


def own_faces(f):
    out = []
    for dim in (1, 2):
        length = f.shape[dim]
        out.append(lax.slice_in_dim(f, length - 2, length, axis=dim))
        out.append(lax.slice_in_dim(f, 0, 2, axis=dim))
    return out


def exchange(faces, zface):
    out = []
    for axis, (last, first) in (("gx", faces[0:2]), ("gy", faces[2:4])):
        n = lax.axis_size(axis)
        out.append(lax.ppermute(last, axis, shift_pairs(n, 1)))
        out.append(lax.ppermute(first, axis, shift_pairs(n, -1)))
    n = lax.axis_size("gz")
    out.append(lax.ppermute(zface, "gz", shift_pairs(n, 1)))
    out.append(lax.ppermute(zface, "gz", shift_pairs(n, -1)))
    return out


def stage(f, rims, potential, orbitals=None):
    norb, cx, cy, cz = f.shape
    last = orbitals is not None
    blk = pl.BlockSpec((BLOCK, cx, cy, cz), lambda i: (i, 0, 0, 0))
    xblk = pl.BlockSpec((BLOCK, 2, cy, cz), lambda i: (i, 0, 0, 0))
    yblk = pl.BlockSpec((BLOCK, cx, 2, cz), lambda i: (i, 0, 0, 0))
    fblk = pl.BlockSpec((cx * cy, 4 * norb), lambda i: (0, 0))
    pblk = pl.BlockSpec((cx, cy, cz), lambda i: (0, 0, 0))
    in_specs = [blk, xblk, xblk, yblk, yblk, fblk, fblk, pblk]
    args = [f, *rims, potential]
    if last:
        in_specs.append(blk)
        args.append(orbitals)
        out_specs = blk
        out_shape = jax.ShapeDtypeStruct(f.shape, jnp.float32)
    else:
        out_specs = (blk, fblk, xblk, xblk, yblk, yblk)
        out_shape = (jax.ShapeDtypeStruct(f.shape, jnp.float32),
                     jax.ShapeDtypeStruct((cx * cy, 4 * norb), jnp.float32),
                     jax.ShapeDtypeStruct((norb, 2, cy, cz), jnp.float32),
                     jax.ShapeDtypeStruct((norb, 2, cy, cz), jnp.float32),
                     jax.ShapeDtypeStruct((norb, cx, 2, cz), jnp.float32),
                     jax.ShapeDtypeStruct((norb, cx, 2, cz), jnp.float32))
    return pl.pallas_call(
        functools.partial(stage_kernel, last=last), grid=(norb // BLOCK,), in_specs=in_specs,
        out_specs=out_specs, out_shape=out_shape, interpret=INTERPRET,
        compiler_params=pltpu.CompilerParams(dimension_semantics=("arbitrary",)),
    )(*args)


def solve_kernel(l_ref, y_ref, o_ref):
    n = y_ref.shape[0]
    for j in range(n):
        acc = y_ref[j]
        other = None
        for k in range(j):
            term = l_ref[j, k] * o_ref[k]
            if k % 2 == 0:
                acc = acc - term
            else:
                other = term if other is None else other + term
        if other is not None:
            acc = acc - other
        o_ref[j] = acc / l_ref[j, j]


def solve_lower(lower, y):
    norb, cx, cy, cz = y.shape
    xb = 4
    blk = pl.BlockSpec((norb, xb, cy, cz), lambda i: (0, i, 0, 0))
    return pl.pallas_call(
        solve_kernel, grid=(cx // xb,),
        in_specs=[pl.BlockSpec(memory_space=pltpu.SMEM), blk], out_specs=blk,
        out_shape=jax.ShapeDtypeStruct(y.shape, jnp.float32), interpret=INTERPRET,
    )(lower, y)


def gram_kernel(y_ref, o_ref, acc_ref):
    n, xb, cy, cz = y_ref.shape
    step = pl.program_id(0)

    @pl.when(step == 0)
    def _():
        acc_ref[...] = jnp.zeros(acc_ref.shape, jnp.float32)

    idx = 0
    for a in range(n):
        ya = y_ref[a].reshape(xb * cy // 8, 8, cz)
        for b in range(a, n):
            yb = y_ref[b].reshape(xb * cy // 8, 8, cz)
            acc_ref[idx] += (ya * yb).sum(axis=0)
            idx += 1

    @pl.when(step == pl.num_programs(0) - 1)
    def _():
        idx = 0
        for a in range(n):
            for b in range(a, n):
                row = jnp.sum(acc_ref[idx], axis=0, keepdims=True)
                o_ref[pl.ds(a * n + b, 1), :] = row
                if b != a:
                    o_ref[pl.ds(b * n + a, 1), :] = row
                idx += 1


def gram(y):
    norb, cx, cy, cz = y.shape
    xb = 4
    pairs = norb * (norb + 1) // 2
    lanes = pl.pallas_call(
        gram_kernel, grid=(cx // xb,),
        in_specs=[pl.BlockSpec((norb, xb, cy, cz), lambda i: (0, i, 0, 0))],
        out_specs=pl.BlockSpec((norb * norb, cz), lambda i: (0, 0)),
        out_shape=jax.ShapeDtypeStruct((norb * norb, cz), jnp.float32),
        scratch_shapes=[pltpu.VMEM((pairs, 8, cz), jnp.float32)], interpret=INTERPRET,
        compiler_params=pltpu.CompilerParams(dimension_semantics=("arbitrary",)),
    )(y)
    return lanes.sum(axis=1).reshape(norb, norb)


def butterfly_sum(c):
    for axis in ("gz", "gy", "gx"):
        n = lax.axis_size(axis)
        d = 1
        while d < n:
            c = c + lax.ppermute(c, axis, [(i, i ^ d) for i in range(n)])
            d *= 2
    return c


def per_device(orbitals, potential):
    first, first_z, *first_faces = stage(orbitals, exchange(own_faces(orbitals), z_faces(orbitals)), potential)
    second = stage(first, exchange(first_faces, first_z), potential, orbitals)
    norb_count = orbitals.shape[0]
    all_cells = second[0].size * lax.axis_size("gx") * lax.axis_size("gy") * lax.axis_size("gz")
    correlation = gram(second) / all_cells
    lower = jnp.linalg.cholesky(butterfly_sum(correlation))
    basis = solve_lower(lower, second)
    return (basis, lower.T)


def solution(mesh):
    in_specs = (P(None, "gx", "gy", "gz"), P("gx", "gy", "gz"))
    out_specs = (P(None, "gx", "gy", "gz"), P())
    return jax.shard_map(
        per_device, mesh=mesh, in_specs=in_specs, out_specs=out_specs, check_vma=False
    )
```

```python
import functools

import jax
import jax.numpy as jnp
from jax import lax
from jax.experimental import pallas as pl
from jax.experimental.pallas import tpu as pltpu
from jax.sharding import PartitionSpec as P

TAPS = (-1.0 / 12.0, 4.0 / 3.0, -2.5, 4.0 / 3.0, -1.0 / 12.0)
BLOCK = 16
INTERPRET = False
HI = lax.Precision.HIGHEST


def shift_pairs(n, step):
    return [(i, (i + step) % n) for i in range(n)]


def face_lanes(plane, orbital, lane, packed):
    cz = plane.shape[1]
    rolled = pltpu.roll(plane, (4 * orbital + 2) % cz, 1)
    return jnp.where(lane // 4 == orbital, rolled, packed)


def stage_kernel(*refs, last):
    if last:
        (f_ref, xlo_ref, xhi_ref, ylo_ref, yhi_ref, zlo_ref, zhi_ref, pot_ref, orb_ref,
         out_ref) = refs
    else:
        (f_ref, xlo_ref, xhi_ref, ylo_ref, yhi_ref, zlo_ref, zhi_ref, pot_ref,
         out_ref, face_ref, xl_ref, xf_ref, yl_ref, yf_ref) = refs
    nb, cx, cy, cz = f_ref.shape
    rows = cx * cy
    step = pl.program_id(0)
    lane = lax.broadcasted_iota(jnp.int32, (rows, cz), 1)
    yid = lax.broadcasted_iota(jnp.int32, (cx, cy, cz), 1)
    pot = pot_ref[...]
    zlo = zlo_ref[...]
    zhi = zhi_ref[...]
    if not last:
        @pl.when(step == 0)
        def _():
            face_ref[...] = jnp.zeros(face_ref.shape, jnp.float32)
        packed = face_ref[...]
    for b in range(nb):
        orbital = step * nb + b
        f3 = f_ref[b]
        summed = 3.0 * TAPS[2] * f3
        ext = jnp.concatenate([xlo_ref[b], f3, xhi_ref[b]], axis=0)
        for offset, weight in ((-2, TAPS[0]), (-1, TAPS[1]), (1, TAPS[3]), (2, TAPS[4])):
            summed = summed + weight * ext[2 + offset: 2 + offset + cx]
        ylo = ylo_ref[b]
        yhi = yhi_ref[b]
        ym2 = jnp.where(yid == 0, ylo[:, 0:1, :], jnp.where(yid == 1, ylo[:, 1:2, :], pltpu.roll(f3, 2, 1)))
        ym1 = jnp.where(yid == 0, ylo[:, 1:2, :], pltpu.roll(f3, 1, 1))
        yp1 = jnp.where(yid == cy - 1, yhi[:, 0:1, :], pltpu.roll(f3, cy - 1, 1))
        yp2 = jnp.where(yid == cy - 2, yhi[:, 0:1, :], jnp.where(yid == cy - 1, yhi[:, 1:2, :], pltpu.roll(f3, cy - 2, 1)))
        for shifted, weight in ((ym2, TAPS[0]), (ym1, TAPS[1]), (yp1, TAPS[3]), (yp2, TAPS[4])):
            summed = summed + weight * shifted
        f2 = f3.reshape(rows, cz)
        base = 4 * orbital
        zm2 = jnp.where(lane < 2, pltpu.roll(zlo, (cz - base) % cz, 1), pltpu.roll(f2, 2, 1))
        zm1 = jnp.where(lane < 1, pltpu.roll(zlo, cz - 1 - base, 1), pltpu.roll(f2, 1, 1))
        zp1 = jnp.where(lane >= cz - 1, pltpu.roll(zhi, cz - 3 - base, 1), pltpu.roll(f2, cz - 1, 1))
        zp2 = jnp.where(lane >= cz - 2, pltpu.roll(zhi, cz - 4 - base, 1), pltpu.roll(f2, cz - 2, 1))
        summed = summed.reshape(rows, cz)
        for shifted, weight in ((zm2, TAPS[0]), (zm1, TAPS[1]), (zp1, TAPS[3]), (zp2, TAPS[4])):
            summed = summed + weight * shifted
        pot2 = pot.reshape(rows, cz)
        h = -0.5 * summed + pot2 * f2
        if last:
            res = 2.0 * (h - 5.5 * f2) / 3.5 - orb_ref[b].reshape(rows, cz)
        else:
            res = (h - 5.5 * f2) / 3.5
            packed = face_lanes(res, orbital, lane, packed)
        res3 = res.reshape(cx, cy, cz)
        out_ref[b] = res3
        if not last:
            xl_ref[b] = res3[cx - 2:]
            xf_ref[b] = res3[:2]
            yl_ref[b] = res3[:, cy - 2:, :]
            yf_ref[b] = res3[:, :2, :]
    if not last:
        face_ref[...] = packed


def z_face_kernel(f_ref, face_ref):
    nb, cx, cy, cz = f_ref.shape
    step = pl.program_id(0)
    lane = lax.broadcasted_iota(jnp.int32, (cx * cy, cz), 1)

    @pl.when(step == 0)
    def _():
        face_ref[...] = jnp.zeros(face_ref.shape, jnp.float32)

    packed = face_ref[...]
    for b in range(nb):
        packed = face_lanes(f_ref[b].reshape(cx * cy, cz), step * nb + b, lane, packed)
    face_ref[...] = packed


def z_faces(f):
    norb, cx, cy, cz = f.shape
    blk = pl.BlockSpec((BLOCK, cx, cy, cz), lambda i: (i, 0, 0, 0))
    fblk = pl.BlockSpec((cx * cy, 4 * norb), lambda i: (0, 0))
    return pl.pallas_call(
        z_face_kernel, grid=(norb // BLOCK,), in_specs=[blk], out_specs=fblk,
        out_shape=jax.ShapeDtypeStruct((cx * cy, 4 * norb), jnp.float32), interpret=INTERPRET,
        compiler_params=pltpu.CompilerParams(dimension_semantics=("arbitrary",)),
    )(f)


def own_faces(f):
    out = []
    for dim in (1, 2):
        length = f.shape[dim]
        out.append(lax.slice_in_dim(f, length - 2, length, axis=dim))
        out.append(lax.slice_in_dim(f, 0, 2, axis=dim))
    return out


def exchange(faces, zface):
    out = []
    for axis, (last, first) in (("gx", faces[0:2]), ("gy", faces[2:4])):
        n = lax.axis_size(axis)
        out.append(lax.ppermute(last, axis, shift_pairs(n, 1)))
        out.append(lax.ppermute(first, axis, shift_pairs(n, -1)))
    n = lax.axis_size("gz")
    out.append(lax.ppermute(zface, "gz", shift_pairs(n, 1)))
    out.append(lax.ppermute(zface, "gz", shift_pairs(n, -1)))
    return out


def stage(f, rims, potential, orbitals=None):
    norb, cx, cy, cz = f.shape
    last = orbitals is not None
    blk = pl.BlockSpec((BLOCK, cx, cy, cz), lambda i: (i, 0, 0, 0))
    xblk = pl.BlockSpec((BLOCK, 2, cy, cz), lambda i: (i, 0, 0, 0))
    yblk = pl.BlockSpec((BLOCK, cx, 2, cz), lambda i: (i, 0, 0, 0))
    fblk = pl.BlockSpec((cx * cy, 4 * norb), lambda i: (0, 0))
    pblk = pl.BlockSpec((cx, cy, cz), lambda i: (0, 0, 0))
    in_specs = [blk, xblk, xblk, yblk, yblk, fblk, fblk, pblk]
    args = [f, *rims, potential]
    if last:
        in_specs.append(blk)
        args.append(orbitals)
        out_specs = blk
        out_shape = jax.ShapeDtypeStruct(f.shape, jnp.float32)
    else:
        out_specs = (blk, fblk, xblk, xblk, yblk, yblk)
        out_shape = (jax.ShapeDtypeStruct(f.shape, jnp.float32),
                     jax.ShapeDtypeStruct((cx * cy, 4 * norb), jnp.float32),
                     jax.ShapeDtypeStruct((norb, 2, cy, cz), jnp.float32),
                     jax.ShapeDtypeStruct((norb, 2, cy, cz), jnp.float32),
                     jax.ShapeDtypeStruct((norb, cx, 2, cz), jnp.float32),
                     jax.ShapeDtypeStruct((norb, cx, 2, cz), jnp.float32))
    return pl.pallas_call(
        functools.partial(stage_kernel, last=last), grid=(norb // BLOCK,), in_specs=in_specs,
        out_specs=out_specs, out_shape=out_shape, interpret=INTERPRET,
        compiler_params=pltpu.CompilerParams(dimension_semantics=("arbitrary",)),
    )(*args)


def solve_kernel(l_ref, y_ref, o_ref):
    n = y_ref.shape[0]
    for j in range(n):
        acc = y_ref[j]
        other = None
        for k in range(j):
            term = l_ref[j, k] * o_ref[k]
            if k % 2 == 0:
                acc = acc - term
            else:
                other = term if other is None else other + term
        if other is not None:
            acc = acc - other
        o_ref[j] = acc / l_ref[j, j]


def solve_lower(lower, y):
    norb, cx, cy, cz = y.shape
    xb = 4
    blk = pl.BlockSpec((norb, xb, cy, cz), lambda i: (0, i, 0, 0))
    return pl.pallas_call(
        solve_kernel, grid=(cx // xb,),
        in_specs=[pl.BlockSpec(memory_space=pltpu.SMEM), blk], out_specs=blk,
        out_shape=jax.ShapeDtypeStruct(y.shape, jnp.float32), interpret=INTERPRET,
    )(lower, y)


def gram_kernel(y_ref, o_ref, acc_ref):
    n, xb, cy, cz = y_ref.shape
    step = pl.program_id(0)

    @pl.when(step == 0)
    def _():
        acc_ref[...] = jnp.zeros(acc_ref.shape, jnp.float32)

    idx = 0
    for a in range(n):
        ya = y_ref[a].reshape(xb * cy // 8, 8, cz)
        for b in range(a, n):
            yb = y_ref[b].reshape(xb * cy // 8, 8, cz)
            acc_ref[idx] += (ya * yb).sum(axis=0)
            idx += 1

    @pl.when(step == pl.num_programs(0) - 1)
    def _():
        idx = 0
        for a in range(n):
            for b in range(a, n):
                row = jnp.sum(acc_ref[idx], axis=0, keepdims=True)
                o_ref[pl.ds(a * n + b, 1), :] = row
                if b != a:
                    o_ref[pl.ds(b * n + a, 1), :] = row
                idx += 1


def gram(y):
    norb, cx, cy, cz = y.shape
    xb = 4
    pairs = norb * (norb + 1) // 2
    lanes = pl.pallas_call(
        gram_kernel, grid=(cx // xb,),
        in_specs=[pl.BlockSpec((norb, xb, cy, cz), lambda i: (0, i, 0, 0))],
        out_specs=pl.BlockSpec((norb * norb, cz), lambda i: (0, 0)),
        out_shape=jax.ShapeDtypeStruct((norb * norb, cz), jnp.float32),
        scratch_shapes=[pltpu.VMEM((pairs, 8, cz), jnp.float32)], interpret=INTERPRET,
        compiler_params=pltpu.CompilerParams(dimension_semantics=("arbitrary",)),
    )(y)
    return lanes.sum(axis=1).reshape(norb, norb)


def butterfly_sum(c):
    for axis in ("gz", "gy", "gx"):
        n = lax.axis_size(axis)
        d = 1
        while d < n:
            c = c + lax.ppermute(c, axis, [(i, i ^ d) for i in range(n)])
            d *= 2
    return c


def per_device(orbitals, potential):
    first, first_z, *first_faces = stage(orbitals, exchange(own_faces(orbitals), z_faces(orbitals)), potential)
    second = stage(first, exchange(first_faces, first_z), potential, orbitals)
    norb_count = orbitals.shape[0]
    all_cells = second[0].size * lax.axis_size("gx") * lax.axis_size("gy") * lax.axis_size("gz")
    correlation = gram(second) / all_cells
    lower = jnp.linalg.cholesky(butterfly_sum(correlation))
    basis = solve_lower(lower, second)
    return (basis, lower.T)


def solution(mesh):
    in_specs = (P(None, "gx", "gy", "gz"), P("gx", "gy", "gz"))
    out_specs = (P(None, "gx", "gy", "gz"), P())
    return jax.shard_map(
        per_device, mesh=mesh, in_specs=in_specs, out_specs=out_specs, check_vma=False
    )
```

```python
import functools

import jax
import jax.numpy as jnp
from jax import lax
from jax.experimental import pallas as pl
from jax.experimental.pallas import tpu as pltpu
from jax.sharding import PartitionSpec as P

TAPS = (-1.0 / 12.0, 4.0 / 3.0, -2.5, 4.0 / 3.0, -1.0 / 12.0)
BLOCK = 16
INTERPRET = False
HI = lax.Precision.HIGHEST


def shift_pairs(n, step):
    return [(i, (i + step) % n) for i in range(n)]


def face_lanes(plane, orbital, lane, packed):
    cz = plane.shape[1]
    rolled = pltpu.roll(plane, (4 * orbital + 2) % cz, 1)
    return jnp.where(lane // 4 == orbital, rolled, packed)


def stage_kernel(*refs, last):
    if last:
        (f_ref, xlo_ref, xhi_ref, ylo_ref, yhi_ref, zlo_ref, zhi_ref, pot_ref, orb_ref,
         out_ref) = refs
    else:
        (f_ref, xlo_ref, xhi_ref, ylo_ref, yhi_ref, zlo_ref, zhi_ref, pot_ref,
         out_ref, face_ref, xl_ref, xf_ref, yl_ref, yf_ref) = refs
    nb, cx, cy, cz = f_ref.shape
    rows = cx * cy
    step = pl.program_id(0)
    lane = lax.broadcasted_iota(jnp.int32, (rows, cz), 1)
    yid = lax.broadcasted_iota(jnp.int32, (cx, cy, cz), 1)
    pot = pot_ref[...]
    zlo = zlo_ref[...]
    zhi = zhi_ref[...]
    if not last:
        @pl.when(step == 0)
        def _():
            face_ref[...] = jnp.zeros(face_ref.shape, jnp.float32)
        packed = face_ref[...]
    for b in range(nb):
        orbital = step * nb + b
        f3 = f_ref[b]
        summed = 3.0 * TAPS[2] * f3
        ext = jnp.concatenate([xlo_ref[b], f3, xhi_ref[b]], axis=0)
        for offset, weight in ((-2, TAPS[0]), (-1, TAPS[1]), (1, TAPS[3]), (2, TAPS[4])):
            summed = summed + weight * ext[2 + offset: 2 + offset + cx]
        ylo = ylo_ref[b]
        yhi = yhi_ref[b]
        ym2 = jnp.where(yid == 0, ylo[:, 0:1, :], jnp.where(yid == 1, ylo[:, 1:2, :], pltpu.roll(f3, 2, 1)))
        ym1 = jnp.where(yid == 0, ylo[:, 1:2, :], pltpu.roll(f3, 1, 1))
        yp1 = jnp.where(yid == cy - 1, yhi[:, 0:1, :], pltpu.roll(f3, cy - 1, 1))
        yp2 = jnp.where(yid == cy - 2, yhi[:, 0:1, :], jnp.where(yid == cy - 1, yhi[:, 1:2, :], pltpu.roll(f3, cy - 2, 1)))
        for shifted, weight in ((ym2, TAPS[0]), (ym1, TAPS[1]), (yp1, TAPS[3]), (yp2, TAPS[4])):
            summed = summed + weight * shifted
        f2 = f3.reshape(rows, cz)
        base = 4 * orbital
        zm2 = jnp.where(lane < 2, pltpu.roll(zlo, (cz - base) % cz, 1), pltpu.roll(f2, 2, 1))
        zm1 = jnp.where(lane < 1, pltpu.roll(zlo, cz - 1 - base, 1), pltpu.roll(f2, 1, 1))
        zp1 = jnp.where(lane >= cz - 1, pltpu.roll(zhi, cz - 3 - base, 1), pltpu.roll(f2, cz - 1, 1))
        zp2 = jnp.where(lane >= cz - 2, pltpu.roll(zhi, cz - 4 - base, 1), pltpu.roll(f2, cz - 2, 1))
        summed = summed.reshape(rows, cz)
        for shifted, weight in ((zm2, TAPS[0]), (zm1, TAPS[1]), (zp1, TAPS[3]), (zp2, TAPS[4])):
            summed = summed + weight * shifted
        pot2 = pot.reshape(rows, cz)
        h = -0.5 * summed + pot2 * f2
        if last:
            res = 2.0 * (h - 5.5 * f2) / 3.5 - orb_ref[b].reshape(rows, cz)
        else:
            res = (h - 5.5 * f2) / 3.5
            packed = face_lanes(res, orbital, lane, packed)
        res3 = res.reshape(cx, cy, cz)
        out_ref[b] = res3
        if not last:
            xl_ref[b] = res3[cx - 2:]
            xf_ref[b] = res3[:2]
            yl_ref[b] = res3[:, cy - 2:, :]
            yf_ref[b] = res3[:, :2, :]
    if not last:
        face_ref[...] = packed


def z_face_kernel(f_ref, face_ref):
    nb, cx, cy, cz = f_ref.shape
    step = pl.program_id(0)
    lane = lax.broadcasted_iota(jnp.int32, (cx * cy, cz), 1)

    @pl.when(step == 0)
    def _():
        face_ref[...] = jnp.zeros(face_ref.shape, jnp.float32)

    packed = face_ref[...]
    for b in range(nb):
        packed = face_lanes(f_ref[b].reshape(cx * cy, cz), step * nb + b, lane, packed)
    face_ref[...] = packed


def z_faces(f):
    norb, cx, cy, cz = f.shape
    blk = pl.BlockSpec((BLOCK, cx, cy, cz), lambda i: (i, 0, 0, 0))
    fblk = pl.BlockSpec((cx * cy, 4 * norb), lambda i: (0, 0))
    return pl.pallas_call(
        z_face_kernel, grid=(norb // BLOCK,), in_specs=[blk], out_specs=fblk,
        out_shape=jax.ShapeDtypeStruct((cx * cy, 4 * norb), jnp.float32), interpret=INTERPRET,
        compiler_params=pltpu.CompilerParams(dimension_semantics=("arbitrary",)),
    )(f)


def own_faces(f):
    out = []
    for dim in (1, 2):
        length = f.shape[dim]
        out.append(lax.slice_in_dim(f, length - 2, length, axis=dim))
        out.append(lax.slice_in_dim(f, 0, 2, axis=dim))
    return out


def exchange(faces, zface):
    out = []
    for axis, (last, first) in (("gx", faces[0:2]), ("gy", faces[2:4])):
        n = lax.axis_size(axis)
        out.append(lax.ppermute(last, axis, shift_pairs(n, 1)))
        out.append(lax.ppermute(first, axis, shift_pairs(n, -1)))
    n = lax.axis_size("gz")
    out.append(lax.ppermute(zface, "gz", shift_pairs(n, 1)))
    out.append(lax.ppermute(zface, "gz", shift_pairs(n, -1)))
    return out


def stage(f, rims, potential, orbitals=None):
    norb, cx, cy, cz = f.shape
    last = orbitals is not None
    blk = pl.BlockSpec((BLOCK, cx, cy, cz), lambda i: (i, 0, 0, 0))
    xblk = pl.BlockSpec((BLOCK, 2, cy, cz), lambda i: (i, 0, 0, 0))
    yblk = pl.BlockSpec((BLOCK, cx, 2, cz), lambda i: (i, 0, 0, 0))
    fblk = pl.BlockSpec((cx * cy, 4 * norb), lambda i: (0, 0))
    pblk = pl.BlockSpec((cx, cy, cz), lambda i: (0, 0, 0))
    in_specs = [blk, xblk, xblk, yblk, yblk, fblk, fblk, pblk]
    args = [f, *rims, potential]
    if last:
        in_specs.append(blk)
        args.append(orbitals)
        out_specs = blk
        out_shape = jax.ShapeDtypeStruct(f.shape, jnp.float32)
    else:
        out_specs = (blk, fblk, xblk, xblk, yblk, yblk)
        out_shape = (jax.ShapeDtypeStruct(f.shape, jnp.float32),
                     jax.ShapeDtypeStruct((cx * cy, 4 * norb), jnp.float32),
                     jax.ShapeDtypeStruct((norb, 2, cy, cz), jnp.float32),
                     jax.ShapeDtypeStruct((norb, 2, cy, cz), jnp.float32),
                     jax.ShapeDtypeStruct((norb, cx, 2, cz), jnp.float32),
                     jax.ShapeDtypeStruct((norb, cx, 2, cz), jnp.float32))
    return pl.pallas_call(
        functools.partial(stage_kernel, last=last), grid=(norb // BLOCK,), in_specs=in_specs,
        out_specs=out_specs, out_shape=out_shape, interpret=INTERPRET,
        compiler_params=pltpu.CompilerParams(dimension_semantics=("arbitrary",)),
    )(*args)


def solve_kernel(l_ref, y_ref, o_ref):
    n = y_ref.shape[0]
    for j in range(n):
        acc = y_ref[j]
        other = None
        for k in range(j):
            term = l_ref[j, k] * o_ref[k]
            if k % 2 == 0:
                acc = acc - term
            else:
                other = term if other is None else other + term
        if other is not None:
            acc = acc - other
        o_ref[j] = acc / l_ref[j, j]


def solve_lower(lower, y):
    norb, cx, cy, cz = y.shape
    xb = 4
    blk = pl.BlockSpec((norb, xb, cy, cz), lambda i: (0, i, 0, 0))
    return pl.pallas_call(
        solve_kernel, grid=(cx // xb,),
        in_specs=[pl.BlockSpec(memory_space=pltpu.SMEM), blk], out_specs=blk,
        out_shape=jax.ShapeDtypeStruct(y.shape, jnp.float32), interpret=INTERPRET,
    )(lower, y)


def gram_kernel(y_ref, o_ref, acc_ref):
    n, xb, cy, cz = y_ref.shape
    step = pl.program_id(0)

    @pl.when(step == 0)
    def _():
        acc_ref[...] = jnp.zeros(acc_ref.shape, jnp.float32)

    idx = 0
    for a in range(n):
        ya = y_ref[a].reshape(xb * cy // 8, 8, cz)
        for b in range(a, n):
            yb = y_ref[b].reshape(xb * cy // 8, 8, cz)
            acc_ref[idx] += (ya * yb).sum(axis=0)
            idx += 1

    @pl.when(step == pl.num_programs(0) - 1)
    def _():
        idx = 0
        for a in range(n):
            for b in range(a, n):
                row = jnp.sum(jnp.sum(acc_ref[idx], axis=0, keepdims=True), axis=1, keepdims=True)
                o_ref[pl.ds(a, 1), pl.ds(b, 1)] = row
                if b != a:
                    o_ref[pl.ds(b, 1), pl.ds(a, 1)] = row
                idx += 1


def gram(y):
    norb, cx, cy, cz = y.shape
    xb = 4
    pairs = norb * (norb + 1) // 2
    lanes = pl.pallas_call(
        gram_kernel, grid=(cx // xb,),
        in_specs=[pl.BlockSpec((norb, xb, cy, cz), lambda i: (0, i, 0, 0))],
        out_specs=pl.BlockSpec((norb, norb), lambda i: (0, 0)),
        out_shape=jax.ShapeDtypeStruct((norb, norb), jnp.float32),
        scratch_shapes=[pltpu.VMEM((pairs, 8, cz), jnp.float32)], interpret=INTERPRET,
        compiler_params=pltpu.CompilerParams(dimension_semantics=("arbitrary",)),
    )(y)
    return lanes


def butterfly_sum(c):
    for axis in ("gz", "gy", "gx"):
        n = lax.axis_size(axis)
        d = 1
        while d < n:
            c = c + lax.ppermute(c, axis, [(i, i ^ d) for i in range(n)])
            d *= 2
    return c


def per_device(orbitals, potential):
    first, first_z, *first_faces = stage(orbitals, exchange(own_faces(orbitals), z_faces(orbitals)), potential)
    second = stage(first, exchange(first_faces, first_z), potential, orbitals)
    norb_count = orbitals.shape[0]
    all_cells = second[0].size * lax.axis_size("gx") * lax.axis_size("gy") * lax.axis_size("gz")
    correlation = gram(second) / all_cells
    lower = jnp.linalg.cholesky(butterfly_sum(correlation))
    basis = solve_lower(lower, second)
    return (basis, lower.T)


def solution(mesh):
    in_specs = (P(None, "gx", "gy", "gz"), P("gx", "gy", "gz"))
    out_specs = (P(None, "gx", "gy", "gz"), P())
    return jax.shard_map(
        per_device, mesh=mesh, in_specs=in_specs, out_specs=out_specs, check_vma=False
    )
```
